32 devices in a mesh: surf: 8 (over z, y), vol: 4 (over x, core).
Axes of the slice: x: 2, y: 2, z: 4, core: 2. Of those that a mesh axis runs over, the one named last changes fastest.
Arguments:
- casting: bfloat16 [32768, 128], P(('surf', 'vol')), may hold values from -5 to 5, as said below
- owner: int32 [32768, 1], P(('surf', 'vol')), may hold values from 0 to 31; in each aligned block of 1024 rows (0 to 1023, 1024 to 2047, ...) at most 128 rows name the same one
- face_id: int32 [32768], P(('surf', 'vol')), may hold values from 0 to 2047
- mold_faces: bfloat16 [65536, 128], P(('surf', 'vol')), may hold values from -5 to 5, as said below
- mortar_d: bfloat16 [64, 64], replicated, may hold values from -0.75 to 0.75
- mortar_m: bfloat16 [64, 64], replicated, may hold values from -0.75 to 0.75
- conduct: bfloat16 [128, 128], replicated, may hold values from -0.5 to 0.5
- volume: bfloat16 [65536, 128], P(('surf', 'vol')), may hold values from -6 to 6
Outputs:
- casting_out: bfloat16 [32768, 128], P(('surf', 'vol'))
- mold_out: bfloat16 [65536, 128], P(('surf', 'vol'))
The draws below stay inside these ranges and needn't reach their ends.
Inputs may be any that keep to these rules, and one draw needn't show every extreme that they name: Among the 1024 rows of one device no owner is named more than 128 times, a bound that some block reaches. `casting`: temperatures lie within -5 to 5; conductances lie within 0.3 to 3. `mold_faces`: temperatures lie within -5 to 5; area weights lie within 0.3 to 3.
All inputs are finite; a program needn't handle non-finite values.
Results may differ from the reference program's by a relative error of at most 0.0055.
Values may be sent and summed in bfloat16 or wider, within the bound.
No kernel may reach another device: no remote copies, remote signals or barrier semaphores. Data moves between devices by JAX's collectives and lax.ppermute only.
A program may use at most 64 MiB of HBM per device.

```python
import math
import jax
import jax.numpy as jnp
import numpy as np

NODES = 64
ROW = 128
SEG_DEV = 1024
FACE_DEV = 2048
CAP = 128
SEGS = 32768
FACES = 65536
N_SURF = 8
N_VOL = 4
DEVICES = 32


def surface_rows(key, count):
    first, second = jax.random.split(jax.random.fold_in(key, 7))
    temps = jnp.clip(jax.random.normal(first, (count, NODES), jnp.float32), -5.0, 5.0)
    coeffs = jnp.exp(jax.random.uniform(second, (count, NODES), jnp.float32, math.log(0.3), math.log(3.0)))
    return jnp.concatenate([temps, coeffs], axis=1).astype(jnp.bfloat16)


def draw_casting(key, part):
    return surface_rows(key, SEGS)


def draw_mold_faces(key, part):
    return surface_rows(jax.random.fold_in(key, 11), FACES)


def plant(entries, stream_key, least, top_value):
    extent = entries.shape
    index_at = [jax.random.randint(jax.random.fold_in(stream_key, axis), (), 0, extent[axis]) for axis in range(len(extent))]
    entries = entries.at[tuple(index_at)].set(least)
    longest = extent.index(max(extent))
    index_at[longest] = (index_at[longest] + 1) % extent[longest]
    return entries.at[tuple(index_at)].set(top_value)


def block_scale(key, extent, shards, low, largest):
    def one(position, shards_of):
        steps = jax.random.uniform(jax.random.fold_in(jax.random.fold_in(key, 6), position), (shards_of,), jnp.float32, low / len(shards), largest / len(shards))
        return jnp.repeat(jnp.exp(steps), extent[position] // shards_of).reshape((-1,) + (1,) * (len(extent) - position - 1))

    factor_of = one(*shards[0])
    for cut in shards[1:]:
        factor_of = factor_of * one(*cut)
    return factor_of


def routed_block(own_key, own, number, rows, amount, top, reach, skew):
    sequence = jax.random.permutation(own_key, amount)
    packed, ordinary = shares(amount, rows * top, reach, skew, True), shares(amount, rows * top, reach, skew, False)
    places = jnp.arange(amount)

    def named(tallies, offset_by):
        used = int((tallies > 0).sum())
        fixed = max(1, used // 4)
        moved = fixed + (places - fixed + offset_by * (used - fixed)) % max(1, amount - fixed)
        return jnp.zeros((amount,), jnp.int32).at[sequence[jnp.where(places < fixed, places, moved)]].set(jnp.asarray(tallies, jnp.int32))

    tallies = jnp.where(number % 4 == 0, named(packed, number // 4), named(ordinary, number - number // 4 - 1))
    mixed = jax.random.permutation(jax.random.fold_in(own, 3), amount)
    giver, taker = mixed[0:amount // 2 * 2:2], mixed[1:amount // 2 * 2:2]
    room = jnp.minimum(tallies[giver] - 1, reach - tallies[taker]) // 2
    room = jnp.where((giver == sequence[0]) | (taker == sequence[0]) | (tallies[taker] == 0), 0, jnp.maximum(room, 0))
    moved = jax.random.randint(jax.random.fold_in(own, 4), (amount // 2,), 0, 1 << 20) % (room + 1)
    tallies = tallies.at[giver].add(-moved).at[taker].add(moved)
    members = jnp.searchsorted(jnp.cumsum(tallies), jnp.arange(rows * top), side="right").astype(jnp.int32)
    table = members.reshape(top, rows).T
    table = table[jax.random.permutation(jax.random.fold_in(own, 1), rows)]
    offset_by = jax.random.randint(jax.random.fold_in(own, 2), (rows, 1), 0, top)
    return jnp.take_along_axis(table, (jnp.arange(top)[None, :] + offset_by) % top, axis=1)


def shares(amount, total, most, skew, full):
    weights = [(1 << 20) // math.isqrt(rank ** skew) + 1 for rank in range(1, amount + 1)]
    largest = most if full else min(most, max(-(-total // amount), total * weights[0] // sum(weights)))
    least = 1 if total - largest >= amount - 1 else 0
    given, spare = [largest] + [least] * (amount - 1), total - largest - least * (amount - 1)
    while spare > 0:
        candidates = [i for i in range(1, amount) if given[i] < largest] or [i for i in range(1, amount) if given[i] < most]
        pool, left = sum([weights[i] for i in candidates]), spare
        for i in candidates:
            extra = min(most - given[i], max(1, left * weights[i] // pool), spare)
            given[i] = given[i] + extra
            spare = spare - extra
    return np.array(given)


def noise(rng, shape, scale, reach, cuts=(), held_as=jnp.bfloat16):
    loudness = block_scale(rng, shape, cuts, -0.22, 0.18) if cuts else 1.0
    values = jax.random.normal(rng, shape, jnp.float32) * scale * loudness
    return jnp.minimum(jnp.maximum(values, -reach), reach).astype(held_as)


def setup_inputs(seed: int = 0) -> dict:
    keys = jax.random.split(jax.random.key(seed), 9)
    casting = draw_casting(jax.random.fold_in(keys[8], 71), 0)
    owner_keys = jax.random.split(jax.random.fold_in(keys[1], 1), SEGS // SEG_DEV)
    owner_turns = jax.random.permutation(jax.random.fold_in(keys[1], 3), SEGS // SEG_DEV)
    owner = jax.vmap(lambda own, number: routed_block(jax.random.fold_in(keys[1], 2), own, number, SEG_DEV, DEVICES, 1, CAP, 2))(owner_keys, owner_turns).reshape((SEGS, 1))
    face_id = plant(jax.random.randint(keys[2], (SEGS,), 0, FACE_DEV), jax.random.fold_in(keys[2], 1), 0, FACE_DEV - 1).astype(jnp.int32)
    mold_faces = draw_mold_faces(jax.random.fold_in(keys[8], 71), 0)
    mortar_d = noise(keys[4], (NODES, NODES), NODES ** -0.5, 0.75)
    mortar_m = noise(keys[5], (NODES, NODES), NODES ** -0.5, 0.75)
    conduct = noise(keys[6], (ROW, ROW), ROW ** -0.5, 0.5)
    volume = noise(keys[7], (FACES, ROW), 1.0, 6.0, ((0, 32),))
    return dict(casting=casting, owner=owner, face_id=face_id, mold_faces=mold_faces, mortar_d=mortar_d, mortar_m=mortar_m, conduct=conduct, volume=volume)


relax = 0.5


def reference(casting, owner, face_id, mold_faces, mortar_d, mortar_m, conduct, volume):
    paired = owner[:, 0].astype(jnp.int32) * FACE_DEV + face_id.astype(jnp.int32)
    mold_rows = mold_faces[paired]
    stacked = jnp.concatenate([mortar_d.T, -mortar_m.T], axis=0)
    joined = jnp.concatenate([mortar_d, mortar_m], axis=1)
    pair_rows = jnp.concatenate([casting[:, :NODES], mold_rows[:, :NODES]], axis=1)
    gap_jump = jnp.dot(pair_rows, stacked, preferred_element_type=jnp.float32)
    heat_flux = (casting[:, NODES:].astype(jnp.float32) * mold_rows[:, NODES:].astype(jnp.float32) * gap_jump).astype(jnp.bfloat16)
    projected = jnp.dot(heat_flux, joined, preferred_element_type=jnp.float32)
    casting_out = jnp.concatenate([projected[:, :NODES], gap_jump], axis=1).astype(jnp.bfloat16)
    gained = projected[:, NODES:].astype(jnp.bfloat16)
    totals = jax.ops.segment_sum(gained.astype(jnp.float32), paired, num_segments=FACES).astype(jnp.bfloat16)
    quarter = FACE_DEV // N_VOL
    placed = totals.reshape(N_SURF, N_VOL, N_VOL, quarter, NODES).transpose(0, 2, 1, 3, 4).reshape(FACES, NODES)
    heat = jnp.dot(volume, conduct, preferred_element_type=jnp.float32)
    inject = jnp.concatenate([placed.astype(jnp.float32), jnp.zeros((FACES, NODES), jnp.float32)], axis=1)
    mold_out = (volume.astype(jnp.float32) + relax * (inject - heat)).astype(jnp.bfloat16)
    return casting_out, mold_out
```

```python
import jax
import jax.numpy as jnp
from jax import lax
from jax.sharding import PartitionSpec as P

relax = 0.5


def contact(rows, mold_rows, stacked, joined, node_count):
    pair_rows = jnp.concatenate([rows[:, :node_count], mold_rows[:, :node_count]], axis=1)
    gap_jump = jnp.dot(pair_rows, stacked, preferred_element_type=jnp.float32)
    heat_flux = (
        rows[:, node_count:].astype(jnp.float32)
        * mold_rows[:, node_count:].astype(jnp.float32)
        * gap_jump
    ).astype(jnp.bfloat16)
    projected = jnp.dot(heat_flux, joined, preferred_element_type=jnp.float32)
    answer = jnp.concatenate([projected[:, :node_count], gap_jump], axis=1).astype(jnp.bfloat16)
    gained = projected[:, node_count:].astype(jnp.bfloat16)
    return (answer, gained)


def local(casting, owner, face_id, mold_faces, mortar_d, mortar_m, conduct, volume):
    seg_rows, row_width = casting.shape
    node_count = mortar_d.shape[0]
    face_rows = mold_faces.shape[0]
    surf_count = lax.axis_size("surf")
    vol_count = lax.axis_size("vol")
    devices = surf_count * vol_count
    capacity = 4 * seg_rows // devices
    slots = devices * capacity
    axes = ("surf", "vol")
    f32, bf16 = jnp.float32, jnp.bfloat16

    target = owner[:, 0]
    hits = (target[:, None] == jnp.arange(devices, dtype=jnp.int32)[None, :]).astype(bf16)
    row_i = lax.broadcasted_iota(jnp.int32, (seg_rows, seg_rows), 0)
    row_j = lax.broadcasted_iota(jnp.int32, (seg_rows, seg_rows), 1)
    earlier = (row_j < row_i).astype(bf16)
    before = jnp.dot(earlier, hits, preferred_element_type=f32)
    position = jnp.sum(before * hits.astype(f32), axis=1).astype(jnp.int32)
    slot_index = target * capacity + position

    code = face_id + 1
    pos_hot = (position[:, None] == jnp.arange(capacity, dtype=jnp.int32)[None, :]).astype(bf16)
    hi = (code // 64).astype(bf16)[:, None]
    lo = (code % 64).astype(bf16)[:, None]
    placed_hi = lax.dot_general(hits, pos_hot * hi, (((0,), (0,)), ((), ())), preferred_element_type=f32)
    placed_lo = lax.dot_general(hits, pos_hot * lo, (((0,), (0,)), ((), ())), preferred_element_type=f32)
    send_ids = (placed_hi * 64.0 + placed_lo).astype(jnp.int32) - 1

    got_ids = lax.all_to_all(send_ids, axes, 0, 0, tiled=True).reshape(slots)

    face_range = jnp.arange(face_rows, dtype=jnp.int32)
    selector = (got_ids[:, None] == face_range[None, :]).astype(bf16)
    ask_rows = jnp.dot(selector, mold_faces, preferred_element_type=f32).astype(bf16)
    back_rows = lax.all_to_all(
        ask_rows.reshape(devices, capacity, row_width), axes, 0, 0, tiled=True
    ).reshape(slots, row_width)
    mold_rows = jnp.take(back_rows, slot_index, axis=0)

    stacked = jnp.concatenate([mortar_d.T, -mortar_m.T], axis=0)
    joined = jnp.concatenate([mortar_d, mortar_m], axis=1)
    casting_out, gained = contact(casting, mold_rows, stacked, joined, node_count)

    send_gain = jnp.zeros((slots, node_count), bf16).at[slot_index].set(gained)
    got_gain = lax.all_to_all(
        send_gain.reshape(devices, capacity, node_count), axes, 0, 0, tiled=True
    ).reshape(slots, node_count)
    totals = lax.dot_general(
        selector, got_gain, (((0,), (0,)), ((), ())), preferred_element_type=f32
    )

    face_totals = totals.astype(bf16)
    quarter = face_rows // vol_count
    relaid = lax.all_to_all(
        face_totals.reshape(vol_count, quarter * node_count // row_width, row_width),
        "vol",
        split_axis=0,
        concat_axis=0,
        tiled=True,
    )
    heat = jnp.dot(volume, conduct, preferred_element_type=f32)
    placed = relaid.reshape(face_rows, node_count).astype(f32)
    inject = jnp.concatenate([placed, jnp.zeros((face_rows, node_count), f32)], axis=1)
    mold_out = (volume.astype(f32) + relax * (inject - heat)).astype(bf16)
    return (casting_out, mold_out)


def solution(mesh):
    return jax.shard_map(
        local,
        mesh=mesh,
        in_specs=(
            P(("surf", "vol"), None),
            P(("surf", "vol"), None),
            P(("surf", "vol")),
            P(("surf", "vol"), None),
            P(),
            P(),
            P(),
            P(("surf", "vol"), None),
        ),
        out_specs=(P(("surf", "vol"), None), P(("surf", "vol"), None)),
        check_vma=False,
    )
```

```python
import jax
import jax.numpy as jnp
from jax import lax
from jax.sharding import PartitionSpec as P

relax = 0.5


def contact(rows, mold_rows, stacked, joined, node_count):
    pair_rows = jnp.concatenate([rows[:, :node_count], mold_rows[:, :node_count]], axis=1)
    gap_jump = jnp.dot(pair_rows, stacked, preferred_element_type=jnp.float32)
    heat_flux = (
        rows[:, node_count:].astype(jnp.float32)
        * mold_rows[:, node_count:].astype(jnp.float32)
        * gap_jump
    ).astype(jnp.bfloat16)
    projected = jnp.dot(heat_flux, joined, preferred_element_type=jnp.float32)
    answer = jnp.concatenate([projected[:, :node_count], gap_jump], axis=1).astype(jnp.bfloat16)
    gained = projected[:, node_count:].astype(jnp.bfloat16)
    return (answer, gained)


def local(casting, owner, face_id, mold_faces, mortar_d, mortar_m, conduct, volume):
    seg_rows, row_width = casting.shape
    node_count = mortar_d.shape[0]
    face_rows = mold_faces.shape[0]
    surf_count = lax.axis_size("surf")
    vol_count = lax.axis_size("vol")
    devices = surf_count * vol_count
    capacity = 4 * seg_rows // devices
    slots = devices * capacity
    axes = ("surf", "vol")
    f32, bf16 = jnp.float32, jnp.bfloat16

    target = owner[:, 0]
    hits = (target[:, None] == jnp.arange(devices, dtype=jnp.int32)[None, :]).astype(bf16)
    row_i = lax.broadcasted_iota(jnp.int32, (seg_rows, seg_rows), 0)
    row_j = lax.broadcasted_iota(jnp.int32, (seg_rows, seg_rows), 1)
    earlier = (row_j < row_i).astype(bf16)
    before = jnp.dot(earlier, hits, preferred_element_type=f32)
    position = jnp.sum(before * hits.astype(f32), axis=1).astype(jnp.int32)
    slot_index = target * capacity + position

    code = face_id + 1
    pos_hot = (position[:, None] == jnp.arange(capacity, dtype=jnp.int32)[None, :]).astype(bf16)
    hi = (code // 64).astype(bf16)[:, None]
    lo = (code % 64).astype(bf16)[:, None]
    placed_hi = lax.dot_general(hits, pos_hot * hi, (((0,), (0,)), ((), ())), preferred_element_type=f32)
    placed_lo = lax.dot_general(hits, pos_hot * lo, (((0,), (0,)), ((), ())), preferred_element_type=f32)
    send_ids = (placed_hi * 64.0 + placed_lo).astype(jnp.int32) - 1

    got_ids = lax.all_to_all(send_ids, axes, 0, 0, tiled=True).reshape(slots)

    face_range = jnp.arange(face_rows, dtype=jnp.int32)
    selector = (got_ids[:, None] == face_range[None, :]).astype(bf16)
    ask_rows = jnp.dot(selector, mold_faces, preferred_element_type=f32).astype(bf16)
    back_rows = lax.all_to_all(
        ask_rows.reshape(devices, capacity, row_width), axes, 0, 0, tiled=True
    ).reshape(slots, row_width)
    mold_rows = jnp.take(back_rows, slot_index, axis=0)

    stacked = jnp.concatenate([mortar_d.T, -mortar_m.T], axis=0)
    joined = jnp.concatenate([mortar_d, mortar_m], axis=1)
    casting_out, gained = contact(casting, mold_rows, stacked, joined, node_count)

    send_gain = jnp.zeros((slots, node_count), bf16).at[slot_index].set(gained)
    got_gain = lax.all_to_all(
        send_gain.reshape(devices, capacity * node_count // row_width, row_width),
        axes, 0, 0, tiled=True,
    ).reshape(slots, node_count)
    totals = lax.dot_general(
        selector, got_gain, (((0,), (0,)), ((), ())), preferred_element_type=f32
    )

    face_totals = totals.astype(bf16)
    quarter = face_rows // vol_count
    relaid = lax.all_to_all(
        face_totals.reshape(vol_count, quarter * node_count // row_width, row_width),
        "vol",
        split_axis=0,
        concat_axis=0,
        tiled=True,
    )
    heat = jnp.dot(volume, conduct, preferred_element_type=f32)
    placed = relaid.reshape(face_rows, node_count).astype(f32)
    inject = jnp.concatenate([placed, jnp.zeros((face_rows, node_count), f32)], axis=1)
    mold_out = (volume.astype(f32) + relax * (inject - heat)).astype(bf16)
    return (casting_out, mold_out)


def solution(mesh):
    return jax.shard_map(
        local,
        mesh=mesh,
        in_specs=(
            P(("surf", "vol"), None),
            P(("surf", "vol"), None),
            P(("surf", "vol")),
            P(("surf", "vol"), None),
            P(),
            P(),
            P(),
            P(("surf", "vol"), None),
        ),
        out_specs=(P(("surf", "vol"), None), P(("surf", "vol"), None)),
        check_vma=False,
    )
```

```python
import jax
import jax.numpy as jnp
from jax import lax
from jax.sharding import PartitionSpec as P

relax = 0.5


def contact(rows, mold_rows, stacked, joined, node_count):
    pair_rows = jnp.concatenate([rows[:, :node_count], mold_rows[:, :node_count]], axis=1)
    gap_jump = jnp.dot(pair_rows, stacked, preferred_element_type=jnp.float32)
    heat_flux = (
        rows[:, node_count:].astype(jnp.float32)
        * mold_rows[:, node_count:].astype(jnp.float32)
        * gap_jump
    ).astype(jnp.bfloat16)
    projected = jnp.dot(heat_flux, joined, preferred_element_type=jnp.float32)
    answer = jnp.concatenate([projected[:, :node_count], gap_jump], axis=1).astype(jnp.bfloat16)
    gained = projected[:, node_count:].astype(jnp.bfloat16)
    return (answer, gained)


def local(casting, owner, face_id, mold_faces, mortar_d, mortar_m, conduct, volume):
    seg_rows, row_width = casting.shape
    node_count = mortar_d.shape[0]
    face_rows = mold_faces.shape[0]
    surf_count = lax.axis_size("surf")
    vol_count = lax.axis_size("vol")
    devices = surf_count * vol_count
    capacity = 4 * seg_rows // devices
    slots = devices * capacity
    axes = ("surf", "vol")
    f32, bf16 = jnp.float32, jnp.bfloat16
    contract0 = (((0,), (0,)), ((), ()))

    target = owner[:, 0]
    hits = (target[:, None] == jnp.arange(devices, dtype=jnp.int32)[None, :]).astype(bf16)
    row_i = lax.broadcasted_iota(jnp.int32, (seg_rows, seg_rows), 0)
    row_j = lax.broadcasted_iota(jnp.int32, (seg_rows, seg_rows), 1)
    earlier = (row_j < row_i).astype(bf16)
    before = jnp.dot(earlier, hits, preferred_element_type=f32)
    position = jnp.sum(before * hits.astype(f32), axis=1).astype(jnp.int32)
    slot_index = target * capacity + position

    code = face_id + 1
    pos_hot = (position[:, None] == jnp.arange(capacity, dtype=jnp.int32)[None, :]).astype(bf16)
    hi = (code // 64).astype(bf16)[:, None]
    lo = (code % 64).astype(bf16)[:, None]
    id_hi = lax.dot_general(hits, pos_hot * hi, contract0, preferred_element_type=f32)
    id_lo = lax.dot_general(hits, pos_hot * lo, contract0, preferred_element_type=f32)
    id_count = 2 * capacity
    id_height = -(-id_count // row_width)
    id_flat = jnp.stack([id_hi, id_lo], axis=1).reshape(devices, id_count)
    id_flat = jnp.pad(id_flat, ((0, 0), (0, id_height * row_width - id_count)))
    id_rows = id_flat.reshape(devices, id_height, row_width)

    send_rows = jnp.zeros((slots, row_width), bf16).at[slot_index].set(casting)
    send = jnp.concatenate(
        [send_rows.reshape(devices, capacity, row_width), id_rows.astype(bf16)], axis=1
    )
    got = lax.all_to_all(send, axes, 0, 0, tiled=True)
    got_rows = got[:, :capacity, :].reshape(slots, row_width)
    got_code = got[:, capacity:, :].astype(f32).reshape(devices, id_height * row_width)
    got_code = got_code[:, :id_count].reshape(devices, 2, capacity)
    got_ids = (got_code[:, 0, :] * 64.0 + got_code[:, 1, :]).astype(jnp.int32).reshape(slots) - 1

    face_range = jnp.arange(face_rows, dtype=jnp.int32)
    selector = (got_ids[:, None] == face_range[None, :]).astype(bf16)
    mold_rows = jnp.dot(selector, mold_faces, preferred_element_type=f32).astype(bf16)

    stacked = jnp.concatenate([mortar_d.T, -mortar_m.T], axis=0)
    joined = jnp.concatenate([mortar_d, mortar_m], axis=1)
    answers, gained = contact(got_rows, mold_rows, stacked, joined, node_count)

    returned = lax.all_to_all(
        answers.reshape(devices, capacity, row_width), axes, 0, 0, tiled=True
    ).reshape(slots, row_width)
    casting_out = jnp.take(returned, slot_index, axis=0)

    totals = lax.dot_general(selector, gained, contract0, preferred_element_type=f32)
    face_totals = totals.astype(bf16)
    quarter = face_rows // vol_count
    relaid = lax.all_to_all(
        face_totals.reshape(vol_count, quarter * node_count // row_width, row_width),
        "vol",
        split_axis=0,
        concat_axis=0,
        tiled=True,
    )
    heat = jnp.dot(volume, conduct, preferred_element_type=f32)
    placed = relaid.reshape(face_rows, node_count).astype(f32)
    inject = jnp.concatenate([placed, jnp.zeros((face_rows, node_count), f32)], axis=1)
    mold_out = (volume.astype(f32) + relax * (inject - heat)).astype(bf16)
    return (casting_out, mold_out)


def solution(mesh):
    return jax.shard_map(
        local,
        mesh=mesh,
        in_specs=(
            P(("surf", "vol"), None),
            P(("surf", "vol"), None),
            P(("surf", "vol")),
            P(("surf", "vol"), None),
            P(),
            P(),
            P(),
            P(("surf", "vol"), None),
        ),
        out_specs=(P(("surf", "vol"), None), P(("surf", "vol"), None)),
        check_vma=False,
    )
```

```python
import jax
import jax.numpy as jnp
from jax import lax
from jax.sharding import PartitionSpec as P

relax = 0.5


def contact(rows, mold_rows, stacked, joined, node_count):
    pair_rows = jnp.concatenate([rows[:, :node_count], mold_rows[:, :node_count]], axis=1)
    gap_jump = jnp.dot(pair_rows, stacked, preferred_element_type=jnp.float32)
    heat_flux = (
        rows[:, node_count:].astype(jnp.float32)
        * mold_rows[:, node_count:].astype(jnp.float32)
        * gap_jump
    ).astype(jnp.bfloat16)
    projected = jnp.dot(heat_flux, joined, preferred_element_type=jnp.float32)
    answer = jnp.concatenate([projected[:, :node_count], gap_jump], axis=1).astype(jnp.bfloat16)
    gained = projected[:, node_count:].astype(jnp.bfloat16)
    return (answer, gained)


def local(casting, owner, face_id, mold_faces, mortar_d, mortar_m, conduct, volume):
    seg_rows, row_width = casting.shape
    node_count = mortar_d.shape[0]
    face_rows = mold_faces.shape[0]
    surf_count = lax.axis_size("surf")
    vol_count = lax.axis_size("vol")
    devices = surf_count * vol_count
    capacity = 4 * seg_rows // devices
    slots = devices * capacity
    axes = ("surf", "vol")
    f32, bf16 = jnp.float32, jnp.bfloat16
    contract0 = (((0,), (0,)), ((), ()))

    target = owner[:, 0]
    hits = (target[:, None] == jnp.arange(devices, dtype=jnp.int32)[None, :]).astype(bf16)
    row_i = lax.broadcasted_iota(jnp.int32, (seg_rows, seg_rows), 0)
    row_j = lax.broadcasted_iota(jnp.int32, (seg_rows, seg_rows), 1)
    earlier = (row_j < row_i).astype(bf16)
    before = jnp.dot(earlier, hits, preferred_element_type=f32)
    position = jnp.sum(before * hits.astype(f32), axis=1).astype(jnp.int32)
    slot_index = target * capacity + position

    code = face_id + 1
    pos_hot = (position[:, None] == jnp.arange(capacity, dtype=jnp.int32)[None, :]).astype(bf16)
    hi = (code // 64).astype(bf16)[:, None]
    lo = (code % 64).astype(bf16)[:, None]
    id_hi = lax.dot_general(hits, pos_hot * hi, contract0, preferred_element_type=f32)
    id_lo = lax.dot_general(hits, pos_hot * lo, contract0, preferred_element_type=f32)
    id_count = 2 * capacity
    id_height = -(-id_count // row_width)
    id_flat = jnp.stack([id_hi, id_lo], axis=1).reshape(devices, id_count)
    id_flat = jnp.pad(id_flat, ((0, 0), (0, id_height * row_width - id_count)))
    id_rows = id_flat.reshape(devices, id_height, row_width)

    send_rows = jnp.zeros((slots, row_width), bf16).at[slot_index].set(casting)
    send = jnp.concatenate(
        [send_rows.reshape(devices, capacity, row_width), id_rows.astype(bf16)], axis=1
    )
    got = lax.all_to_all(send, axes, 0, 0, tiled=True)
    got_rows = got[:, :capacity, :].reshape(slots, row_width)
    got_code = got[:, capacity:, :].astype(f32).reshape(devices, id_height * row_width)
    got_code = got_code[:, :id_count].reshape(devices, 2, capacity)
    got_ids = (got_code[:, 0, :] * 64.0 + got_code[:, 1, :]).astype(jnp.int32).reshape(slots) - 1

    face_range = jnp.arange(face_rows, dtype=jnp.int32)
    selector = (got_ids[:, None] == face_range[None, :]).astype(bf16)
    mold_rows = jnp.dot(selector, mold_faces, preferred_element_type=f32).astype(bf16)

    stacked = jnp.concatenate([mortar_d.T, -mortar_m.T], axis=0)
    joined = jnp.concatenate([mortar_d, mortar_m], axis=1)
    answers, gained = contact(got_rows, mold_rows, stacked, joined, node_count)

    returned = lax.all_to_all(
        answers.reshape(devices, capacity, row_width), axes, 0, 0, tiled=True
    ).reshape(slots, row_width)
    totals = lax.dot_general(selector, gained, contract0, preferred_element_type=f32)
    face_totals, returned = lax.optimization_barrier((totals.astype(bf16), returned))
    casting_out = jnp.take(returned, slot_index, axis=0)

    quarter = face_rows // vol_count
    relaid = lax.all_to_all(
        face_totals.reshape(vol_count, quarter * node_count // row_width, row_width),
        "vol",
        split_axis=0,
        concat_axis=0,
        tiled=True,
    )
    heat = jnp.dot(volume, conduct, preferred_element_type=f32)
    placed = relaid.reshape(face_rows, node_count).astype(f32)
    inject = jnp.concatenate([placed, jnp.zeros((face_rows, node_count), f32)], axis=1)
    mold_out = (volume.astype(f32) + relax * (inject - heat)).astype(bf16)
    return (casting_out, mold_out)


def solution(mesh):
    return jax.shard_map(
        local,
        mesh=mesh,
        in_specs=(
            P(("surf", "vol"), None),
            P(("surf", "vol"), None),
            P(("surf", "vol")),
            P(("surf", "vol"), None),
            P(),
            P(),
            P(),
            P(("surf", "vol"), None),
        ),
        out_specs=(P(("surf", "vol"), None), P(("surf", "vol"), None)),
        check_vma=False,
    )
```

```python
import jax
import jax.numpy as jnp
from jax import lax
from jax.sharding import PartitionSpec as P

relax = 0.5


def contact(rows, mold_rows, stacked, joined, node_count):
    pair_rows = jnp.concatenate([rows[:, :node_count], mold_rows[:, :node_count]], axis=1)
    gap_jump = jnp.dot(pair_rows, stacked, preferred_element_type=jnp.float32)
    heat_flux = (
        rows[:, node_count:].astype(jnp.float32)
        * mold_rows[:, node_count:].astype(jnp.float32)
        * gap_jump
    ).astype(jnp.bfloat16)
    projected = jnp.dot(heat_flux, joined, preferred_element_type=jnp.float32)
    answer = jnp.concatenate([projected[:, :node_count], gap_jump], axis=1).astype(jnp.bfloat16)
    gained = projected[:, node_count:].astype(jnp.bfloat16)
    return (answer, gained)


def local(casting, owner, face_id, mold_faces, mortar_d, mortar_m, conduct, volume):
    seg_rows, row_width = casting.shape
    node_count = mortar_d.shape[0]
    face_rows = mold_faces.shape[0]
    surf_count = lax.axis_size("surf")
    vol_count = lax.axis_size("vol")
    devices = surf_count * vol_count
    capacity = 4 * seg_rows // devices
    slots = devices * capacity
    axes = ("surf", "vol")
    f32, bf16 = jnp.float32, jnp.bfloat16
    contract0 = (((0,), (0,)), ((), ()))

    target = owner[:, 0]
    hits = (target[:, None] == jnp.arange(devices, dtype=jnp.int32)[None, :]).astype(bf16)
    row_i = lax.broadcasted_iota(jnp.int32, (seg_rows, seg_rows), 0)
    row_j = lax.broadcasted_iota(jnp.int32, (seg_rows, seg_rows), 1)
    earlier = (row_j < row_i).astype(bf16)
    before = jnp.dot(earlier, hits, preferred_element_type=f32)
    position = jnp.sum(before * hits.astype(f32), axis=1).astype(jnp.int32)
    slot_index = target * capacity + position

    code = face_id + 1
    pos_hot = (position[:, None] == jnp.arange(capacity, dtype=jnp.int32)[None, :]).astype(bf16)
    hi = (code // 64).astype(bf16)[:, None]
    lo = (code % 64).astype(bf16)[:, None]
    id_hi = lax.dot_general(hits, pos_hot * hi, contract0, preferred_element_type=f32)
    id_lo = lax.dot_general(hits, pos_hot * lo, contract0, preferred_element_type=f32)
    id_count = 2 * capacity
    id_height = -(-id_count // row_width)
    id_flat = jnp.stack([id_hi, id_lo], axis=1).reshape(devices, id_count)
    id_flat = jnp.pad(id_flat, ((0, 0), (0, id_height * row_width - id_count)))
    id_rows = id_flat.reshape(devices, id_height, row_width)

    block = capacity + id_height
    send = jnp.zeros((devices, block, row_width), bf16).at[:, capacity:, :].set(id_rows.astype(bf16))
    send = send.reshape(devices * block, row_width).at[target * block + position].set(casting)
    send = send.reshape(devices, block, row_width)
    got = lax.all_to_all(send, axes, 0, 0, tiled=True)
    got_rows = got[:, :capacity, :].reshape(slots, row_width)
    got_code = got[:, capacity:, :].astype(f32).reshape(devices, id_height * row_width)
    got_code = got_code[:, :id_count].reshape(devices, 2, capacity)
    got_ids = (got_code[:, 0, :] * 64.0 + got_code[:, 1, :]).astype(jnp.int32).reshape(slots) - 1

    face_range = jnp.arange(face_rows, dtype=jnp.int32)
    selector = (got_ids[:, None] == face_range[None, :]).astype(bf16)
    mold_rows = jnp.dot(selector, mold_faces, preferred_element_type=f32).astype(bf16)

    stacked = jnp.concatenate([mortar_d.T, -mortar_m.T], axis=0)
    joined = jnp.concatenate([mortar_d, mortar_m], axis=1)
    answers, gained = contact(got_rows, mold_rows, stacked, joined, node_count)

    returned = lax.all_to_all(
        answers.reshape(devices, capacity, row_width), axes, 0, 0, tiled=True
    ).reshape(slots, row_width)
    totals = lax.dot_general(selector, gained, contract0, preferred_element_type=f32)
    quarter = face_rows // vol_count
    face_totals = totals.astype(bf16).reshape(vol_count, quarter * node_count // row_width, row_width)
    face_totals, returned = lax.optimization_barrier((face_totals, returned))
    casting_out = jnp.take(returned, slot_index, axis=0)

    relaid = lax.all_to_all(
        face_totals,
        "vol",
        split_axis=0,
        concat_axis=0,
        tiled=True,
    )
    heat = jnp.dot(volume, conduct, preferred_element_type=f32)
    placed = relaid.reshape(face_rows, node_count).astype(f32)
    inject = jnp.concatenate([placed, jnp.zeros((face_rows, node_count), f32)], axis=1)
    mold_out = (volume.astype(f32) + relax * (inject - heat)).astype(bf16)
    return (casting_out, mold_out)


def solution(mesh):
    return jax.shard_map(
        local,
        mesh=mesh,
        in_specs=(
            P(("surf", "vol"), None),
            P(("surf", "vol"), None),
            P(("surf", "vol")),
            P(("surf", "vol"), None),
            P(),
            P(),
            P(),
            P(("surf", "vol"), None),
        ),
        out_specs=(P(("surf", "vol"), None), P(("surf", "vol"), None)),
        check_vma=False,
    )
```

```python
import jax
import jax.numpy as jnp
from jax import lax
from jax.sharding import PartitionSpec as P

relax = 0.5


def contact(rows, mold_rows, stacked, joined, node_count):
    pair_rows = jnp.concatenate([rows[:, :node_count], mold_rows[:, :node_count]], axis=1)
    gap_jump = jnp.dot(pair_rows, stacked, preferred_element_type=jnp.float32)
    heat_flux = (
        rows[:, node_count:].astype(jnp.float32)
        * mold_rows[:, node_count:].astype(jnp.float32)
        * gap_jump
    ).astype(jnp.bfloat16)
    projected = jnp.dot(heat_flux, joined, preferred_element_type=jnp.float32)
    answer = jnp.concatenate([projected[:, :node_count], gap_jump], axis=1).astype(jnp.bfloat16)
    gained = projected[:, node_count:].astype(jnp.bfloat16)
    return (answer, gained)


def local(casting, owner, face_id, mold_faces, mortar_d, mortar_m, conduct, volume):
    seg_rows, row_width = casting.shape
    node_count = mortar_d.shape[0]
    face_rows = mold_faces.shape[0]
    surf_count = lax.axis_size("surf")
    vol_count = lax.axis_size("vol")
    devices = surf_count * vol_count
    capacity = 4 * seg_rows // devices
    slots = devices * capacity
    axes = ("surf", "vol")
    f32, bf16 = jnp.float32, jnp.bfloat16
    contract0 = (((0,), (0,)), ((), ()))

    target = owner[:, 0]
    hits = (target[:, None] == jnp.arange(devices, dtype=jnp.int32)[None, :]).astype(bf16)
    row_i = lax.broadcasted_iota(jnp.int32, (seg_rows, seg_rows), 0)
    row_j = lax.broadcasted_iota(jnp.int32, (seg_rows, seg_rows), 1)
    earlier = (row_j < row_i).astype(bf16)
    before = jnp.dot(earlier, hits, preferred_element_type=f32)
    position = jnp.sum(before * hits.astype(f32), axis=1).astype(jnp.int32)
    slot_index = target * capacity + position

    code = face_id + 1
    pos_hot = (position[:, None] == jnp.arange(capacity, dtype=jnp.int32)[None, :]).astype(bf16)
    hi = (code // 64).astype(bf16)[:, None]
    lo = (code % 64).astype(bf16)[:, None]
    id_hi = lax.dot_general(hits, pos_hot * hi, contract0, preferred_element_type=f32)
    id_lo = lax.dot_general(hits, pos_hot * lo, contract0, preferred_element_type=f32)
    id_count = 2 * capacity
    id_height = -(-id_count // row_width)
    id_flat = jnp.stack([id_hi, id_lo], axis=1).reshape(devices, id_count)
    id_flat = jnp.pad(id_flat, ((0, 0), (0, id_height * row_width - id_count)))
    id_rows = id_flat.reshape(devices, id_height, row_width)

    block = -(-(capacity + id_height) // 16) * 16
    send = jnp.zeros((devices, block, row_width), bf16)
    send = send.at[:, capacity:capacity + id_height, :].set(id_rows.astype(bf16))
    send = send.reshape(devices * block, row_width).at[target * block + position].set(casting)
    send = send.reshape(devices, block, row_width)
    got = lax.all_to_all(send, axes, 0, 0, tiled=True)
    got_rows = got[:, :capacity, :].reshape(slots, row_width)
    got_code = got[:, capacity:capacity + id_height, :].astype(f32).reshape(devices, id_height * row_width)
    got_code = got_code[:, :id_count].reshape(devices, 2, capacity)
    got_ids = (got_code[:, 0, :] * 64.0 + got_code[:, 1, :]).astype(jnp.int32).reshape(slots) - 1

    face_range = jnp.arange(face_rows, dtype=jnp.int32)
    selector = (got_ids[:, None] == face_range[None, :]).astype(bf16)
    mold_rows = jnp.dot(selector, mold_faces, preferred_element_type=f32).astype(bf16)

    stacked = jnp.concatenate([mortar_d.T, -mortar_m.T], axis=0)
    joined = jnp.concatenate([mortar_d, mortar_m], axis=1)
    answers, gained = contact(got_rows, mold_rows, stacked, joined, node_count)

    returned = lax.all_to_all(
        answers.reshape(devices, capacity, row_width), axes, 0, 0, tiled=True
    ).reshape(slots, row_width)
    totals = lax.dot_general(selector, gained, contract0, preferred_element_type=f32)
    quarter = face_rows // vol_count
    face_totals = totals.astype(bf16).reshape(vol_count, quarter * node_count // row_width, row_width)
    face_totals, returned = lax.optimization_barrier((face_totals, returned))
    casting_out = jnp.take(returned, slot_index, axis=0)

    relaid = lax.all_to_all(
        face_totals,
        "vol",
        split_axis=0,
        concat_axis=0,
        tiled=True,
    )
    heat = jnp.dot(volume, conduct, preferred_element_type=f32)
    placed = relaid.reshape(face_rows, node_count).astype(f32)
    inject = jnp.concatenate([placed, jnp.zeros((face_rows, node_count), f32)], axis=1)
    mold_out = (volume.astype(f32) + relax * (inject - heat)).astype(bf16)
    return (casting_out, mold_out)


def solution(mesh):
    return jax.shard_map(
        local,
        mesh=mesh,
        in_specs=(
            P(("surf", "vol"), None),
            P(("surf", "vol"), None),
            P(("surf", "vol")),
            P(("surf", "vol"), None),
            P(),
            P(),
            P(),
            P(("surf", "vol"), None),
        ),
        out_specs=(P(("surf", "vol"), None), P(("surf", "vol"), None)),
        check_vma=False,
    )
```

```python
import jax
import jax.numpy as jnp
from jax import lax
from jax.experimental import pallas as pl
from jax.experimental.pallas import tpu as pltpu
from jax.sharding import PartitionSpec as P

relax = 0.5


def contact(rows, mold_rows, stacked, joined, node_count):
    pair_rows = jnp.concatenate([rows[:, :node_count], mold_rows[:, :node_count]], axis=1)
    gap_jump = jnp.dot(pair_rows, stacked, preferred_element_type=jnp.float32)
    heat_flux = (
        rows[:, node_count:].astype(jnp.float32)
        * mold_rows[:, node_count:].astype(jnp.float32)
        * gap_jump
    ).astype(jnp.bfloat16)
    projected = jnp.dot(heat_flux, joined, preferred_element_type=jnp.float32)
    answer = jnp.concatenate([projected[:, :node_count], gap_jump], axis=1).astype(jnp.bfloat16)
    gained = projected[:, node_count:].astype(jnp.bfloat16)
    return (answer, gained)


def owner_kernel(ids_ref, rows_ref, faces_ref, wc_ref, wm_ref, wj_ref, ans_ref, gain_ref):
    blk = ids_ref.shape[0]
    width = faces_ref.shape[1]
    half = gain_ref.shape[1]
    f32, bf16 = jnp.float32, jnp.bfloat16
    ids = ids_ref[...]
    face_iota = lax.broadcasted_iota(jnp.int32, (blk, faces_ref.shape[0]), 1)
    sel = (ids == face_iota).astype(bf16)
    mold = jnp.dot(sel, faces_ref[...], preferred_element_type=f32).astype(bf16)
    rows = rows_ref[...].reshape(blk, width)
    gap = jnp.dot(rows, wc_ref[...], preferred_element_type=f32) + jnp.dot(
        mold, wm_ref[...], preferred_element_type=f32
    )
    flux = (rows.astype(f32) * mold.astype(f32) * gap).astype(bf16)
    projected = jnp.dot(flux, wj_ref[...], preferred_element_type=f32)
    lane = lax.broadcasted_iota(jnp.int32, (blk, width), 1)
    ans_ref[...] = jnp.where(lane < half, projected, gap).astype(bf16)
    gain_ref[...] = projected[:, half:].astype(bf16)


def owner_contact(got, got_ids, mold_faces, mortar_d, mortar_m, capacity):
    devices, _, width = got.shape
    half = mortar_d.shape[0]
    slots = devices * capacity
    face_rows = mold_faces.shape[0]
    blk = 256
    per = blk // capacity
    zero = jnp.zeros((half, half), mortar_d.dtype)
    wc = jnp.block([[zero, mortar_d.T], [zero, zero]])
    wm = jnp.block([[zero, -mortar_m.T], [zero, zero]])
    wj = jnp.block([[zero, zero], [mortar_d, mortar_m]])
    full = lambda i: (0, 0)
    cost = pl.CostEstimate(
        flops=2 * slots * width * (face_rows + 3 * width),
        bytes_accessed=slots * width * 2 * 3 + face_rows * width * 2,
        transcendentals=0,
    )
    return pl.pallas_call(
        owner_kernel,
        grid=(slots // blk,),
        in_specs=[
            pl.BlockSpec((blk, 1), lambda i: (i, 0)),
            pl.BlockSpec((per, capacity, width), lambda i: (i, 0, 0)),
            pl.BlockSpec((face_rows, width), full),
            pl.BlockSpec((width, width), full),
            pl.BlockSpec((width, width), full),
            pl.BlockSpec((width, width), full),
        ],
        out_specs=[
            pl.BlockSpec((blk, width), lambda i: (i, 0)),
            pl.BlockSpec((blk, half), lambda i: (i, 0)),
        ],
        out_shape=[
            jax.ShapeDtypeStruct((slots, width), jnp.bfloat16),
            jax.ShapeDtypeStruct((slots, half), jnp.bfloat16),
        ],
        cost_estimate=cost,
    )(got_ids.reshape(slots, 1), got, mold_faces, wc, wm, wj)


def local(casting, owner, face_id, mold_faces, mortar_d, mortar_m, conduct, volume):
    seg_rows, row_width = casting.shape
    node_count = mortar_d.shape[0]
    face_rows = mold_faces.shape[0]
    surf_count = lax.axis_size("surf")
    vol_count = lax.axis_size("vol")
    devices = surf_count * vol_count
    capacity = 4 * seg_rows // devices
    slots = devices * capacity
    axes = ("surf", "vol")
    f32, bf16 = jnp.float32, jnp.bfloat16
    contract0 = (((0,), (0,)), ((), ()))

    target = owner[:, 0]
    hits = (target[:, None] == jnp.arange(devices, dtype=jnp.int32)[None, :]).astype(bf16)
    row_i = lax.broadcasted_iota(jnp.int32, (seg_rows, seg_rows), 0)
    row_j = lax.broadcasted_iota(jnp.int32, (seg_rows, seg_rows), 1)
    earlier = (row_j < row_i).astype(bf16)
    before = jnp.dot(earlier, hits, preferred_element_type=f32)
    position = jnp.sum(before * hits.astype(f32), axis=1).astype(jnp.int32)
    slot_index = target * capacity + position

    code = face_id + 1
    pos_hot = (position[:, None] == jnp.arange(capacity, dtype=jnp.int32)[None, :]).astype(bf16)
    hi = (code // 64).astype(bf16)[:, None]
    lo = (code % 64).astype(bf16)[:, None]
    id_hi = lax.dot_general(hits, pos_hot * hi, contract0, preferred_element_type=f32)
    id_lo = lax.dot_general(hits, pos_hot * lo, contract0, preferred_element_type=f32)
    id_count = 2 * capacity
    id_height = -(-id_count // row_width)
    id_flat = jnp.stack([id_hi, id_lo], axis=1).reshape(devices, id_count)
    id_flat = jnp.pad(id_flat, ((0, 0), (0, id_height * row_width - id_count)))
    id_rows = id_flat.reshape(devices, id_height, row_width)

    block = capacity + id_height
    send = jnp.zeros((devices, block, row_width), bf16).at[:, capacity:, :].set(id_rows.astype(bf16))
    send = send.reshape(devices * block, row_width).at[target * block + position].set(casting)
    send = send.reshape(devices, block, row_width)
    got = lax.all_to_all(send, axes, 0, 0, tiled=True)
    got_code = got[:, capacity:, :].astype(f32).reshape(devices, id_height * row_width)
    got_code = got_code[:, :id_count].reshape(devices, 2, capacity)
    got_ids = (got_code[:, 0, :] * 64.0 + got_code[:, 1, :]).astype(jnp.int32).reshape(slots) - 1

    answers, gained = owner_contact(got, got_ids, mold_faces, mortar_d, mortar_m, capacity)
    face_range = jnp.arange(face_rows, dtype=jnp.int32)
    selector = (got_ids[:, None] == face_range[None, :]).astype(bf16)

    returned = lax.all_to_all(
        answers.reshape(devices, capacity, row_width), axes, 0, 0, tiled=True
    ).reshape(slots, row_width)
    totals = lax.dot_general(selector, gained, contract0, preferred_element_type=f32)
    quarter = face_rows // vol_count
    face_totals = totals.astype(bf16).reshape(vol_count, quarter * node_count // row_width, row_width)
    face_totals, returned = lax.optimization_barrier((face_totals, returned))
    casting_out = jnp.take(returned, slot_index, axis=0)

    relaid = lax.all_to_all(
        face_totals,
        "vol",
        split_axis=0,
        concat_axis=0,
        tiled=True,
    )
    heat = jnp.dot(volume, conduct, preferred_element_type=f32)
    placed = relaid.reshape(face_rows, node_count).astype(f32)
    inject = jnp.concatenate([placed, jnp.zeros((face_rows, node_count), f32)], axis=1)
    mold_out = (volume.astype(f32) + relax * (inject - heat)).astype(bf16)
    return (casting_out, mold_out)


def solution(mesh):
    return jax.shard_map(
        local,
        mesh=mesh,
        in_specs=(
            P(("surf", "vol"), None),
            P(("surf", "vol"), None),
            P(("surf", "vol")),
            P(("surf", "vol"), None),
            P(),
            P(),
            P(),
            P(("surf", "vol"), None),
        ),
        out_specs=(P(("surf", "vol"), None), P(("surf", "vol"), None)),
        check_vma=False,
    )
```

```python
import jax
import jax.numpy as jnp
from jax import lax
from jax.experimental import pallas as pl
from jax.experimental.pallas import tpu as pltpu
from jax.sharding import PartitionSpec as P

relax = 0.5


def contact(rows, mold_rows, stacked, joined, node_count):
    pair_rows = jnp.concatenate([rows[:, :node_count], mold_rows[:, :node_count]], axis=1)
    gap_jump = jnp.dot(pair_rows, stacked, preferred_element_type=jnp.float32)
    heat_flux = (
        rows[:, node_count:].astype(jnp.float32)
        * mold_rows[:, node_count:].astype(jnp.float32)
        * gap_jump
    ).astype(jnp.bfloat16)
    projected = jnp.dot(heat_flux, joined, preferred_element_type=jnp.float32)
    answer = jnp.concatenate([projected[:, :node_count], gap_jump], axis=1).astype(jnp.bfloat16)
    gained = projected[:, node_count:].astype(jnp.bfloat16)
    return (answer, gained)


def owner_kernel(ids_ref, rows_ref, faces_ref, wc_ref, wm_ref, wj_ref, ans_ref, gain_ref):
    blk = ids_ref.shape[1]
    width = faces_ref.shape[1]
    half = gain_ref.shape[1]
    f32, bf16 = jnp.float32, jnp.bfloat16
    ids = ids_ref[...]
    face_iota = lax.broadcasted_iota(jnp.int32, (faces_ref.shape[0], blk), 0)
    sel_t = (face_iota == ids).astype(bf16)
    mold = lax.dot_general(
        sel_t, faces_ref[...], (((0,), (0,)), ((), ())), preferred_element_type=f32
    ).astype(bf16)
    rows = rows_ref[...].reshape(blk, width)
    gap = jnp.dot(rows, wc_ref[...], preferred_element_type=f32) + jnp.dot(
        mold, wm_ref[...], preferred_element_type=f32
    )
    flux = (rows.astype(f32) * mold.astype(f32) * gap).astype(bf16)
    projected = jnp.dot(flux, wj_ref[...], preferred_element_type=f32)
    lane = lax.broadcasted_iota(jnp.int32, (blk, width), 1)
    ans_ref[...] = jnp.where(lane < half, projected, gap).astype(bf16)
    gain_ref[...] = projected[:, half:].astype(bf16)


def owner_contact(got, got_ids, mold_faces, mortar_d, mortar_m, capacity):
    devices, _, width = got.shape
    half = mortar_d.shape[0]
    slots = devices * capacity
    face_rows = mold_faces.shape[0]
    blk = 256
    per = blk // capacity
    zero = jnp.zeros((half, half), mortar_d.dtype)
    wc = jnp.block([[zero, mortar_d.T], [zero, zero]])
    wm = jnp.block([[zero, -mortar_m.T], [zero, zero]])
    wj = jnp.block([[zero, zero], [mortar_d, mortar_m]])
    full = lambda i: (0, 0)
    cost = pl.CostEstimate(
        flops=2 * slots * width * (face_rows + 3 * width),
        bytes_accessed=slots * width * 2 * 3 + face_rows * width * 2,
        transcendentals=0,
    )
    return pl.pallas_call(
        owner_kernel,
        grid=(slots // blk,),
        in_specs=[
            pl.BlockSpec((1, blk), lambda i: (0, i)),
            pl.BlockSpec((per, capacity, width), lambda i: (i, 0, 0)),
            pl.BlockSpec((face_rows, width), full),
            pl.BlockSpec((width, width), full),
            pl.BlockSpec((width, width), full),
            pl.BlockSpec((width, width), full),
        ],
        out_specs=[
            pl.BlockSpec((blk, width), lambda i: (i, 0)),
            pl.BlockSpec((blk, half), lambda i: (i, 0)),
        ],
        out_shape=[
            jax.ShapeDtypeStruct((slots, width), jnp.bfloat16),
            jax.ShapeDtypeStruct((slots, half), jnp.bfloat16),
        ],
        cost_estimate=cost,
    )(got_ids.reshape(1, slots), got, mold_faces, wc, wm, wj)


def local(casting, owner, face_id, mold_faces, mortar_d, mortar_m, conduct, volume):
    seg_rows, row_width = casting.shape
    node_count = mortar_d.shape[0]
    face_rows = mold_faces.shape[0]
    surf_count = lax.axis_size("surf")
    vol_count = lax.axis_size("vol")
    devices = surf_count * vol_count
    capacity = 4 * seg_rows // devices
    slots = devices * capacity
    axes = ("surf", "vol")
    f32, bf16 = jnp.float32, jnp.bfloat16
    contract0 = (((0,), (0,)), ((), ()))

    target = owner[:, 0]
    hits = (target[:, None] == jnp.arange(devices, dtype=jnp.int32)[None, :]).astype(bf16)
    row_i = lax.broadcasted_iota(jnp.int32, (seg_rows, seg_rows), 0)
    row_j = lax.broadcasted_iota(jnp.int32, (seg_rows, seg_rows), 1)
    earlier = (row_j < row_i).astype(bf16)
    before = jnp.dot(earlier, hits, preferred_element_type=f32)
    position = jnp.sum(before * hits.astype(f32), axis=1).astype(jnp.int32)
    slot_index = target * capacity + position

    code = face_id + 1
    pos_hot = (position[:, None] == jnp.arange(capacity, dtype=jnp.int32)[None, :]).astype(bf16)
    hi = (code // 64).astype(bf16)[:, None]
    lo = (code % 64).astype(bf16)[:, None]
    id_hi = lax.dot_general(hits, pos_hot * hi, contract0, preferred_element_type=f32)
    id_lo = lax.dot_general(hits, pos_hot * lo, contract0, preferred_element_type=f32)
    id_count = 2 * capacity
    id_height = -(-id_count // row_width)
    id_flat = jnp.stack([id_hi, id_lo], axis=1).reshape(devices, id_count)
    id_flat = jnp.pad(id_flat, ((0, 0), (0, id_height * row_width - id_count)))
    id_rows = id_flat.reshape(devices, id_height, row_width)

    block = capacity + id_height
    send = jnp.zeros((devices, block, row_width), bf16).at[:, capacity:, :].set(id_rows.astype(bf16))
    send = send.reshape(devices * block, row_width).at[target * block + position].set(casting)
    send = send.reshape(devices, block, row_width)
    got = lax.all_to_all(send, axes, 0, 0, tiled=True)
    got_code = got[:, capacity:, :].astype(f32).reshape(devices, id_height * row_width)
    got_code = got_code[:, :id_count].reshape(devices, 2, capacity)
    got_ids = (got_code[:, 0, :] * 64.0 + got_code[:, 1, :]).astype(jnp.int32).reshape(slots) - 1

    answers, gained = owner_contact(got, got_ids, mold_faces, mortar_d, mortar_m, capacity)
    face_range = jnp.arange(face_rows, dtype=jnp.int32)
    selector = (got_ids[:, None] == face_range[None, :]).astype(bf16)

    returned = lax.all_to_all(
        answers.reshape(devices, capacity, row_width), axes, 0, 0, tiled=True
    ).reshape(slots, row_width)
    totals = lax.dot_general(selector, gained, contract0, preferred_element_type=f32)
    quarter = face_rows // vol_count
    face_totals = totals.astype(bf16).reshape(vol_count, quarter * node_count // row_width, row_width)
    face_totals, returned = lax.optimization_barrier((face_totals, returned))
    casting_out = jnp.take(returned, slot_index, axis=0)

    relaid = lax.all_to_all(
        face_totals,
        "vol",
        split_axis=0,
        concat_axis=0,
        tiled=True,
    )
    heat = jnp.dot(volume, conduct, preferred_element_type=f32)
    placed = relaid.reshape(face_rows, node_count).astype(f32)
    inject = jnp.concatenate([placed, jnp.zeros((face_rows, node_count), f32)], axis=1)
    mold_out = (volume.astype(f32) + relax * (inject - heat)).astype(bf16)
    return (casting_out, mold_out)


def solution(mesh):
    return jax.shard_map(
        local,
        mesh=mesh,
        in_specs=(
            P(("surf", "vol"), None),
            P(("surf", "vol"), None),
            P(("surf", "vol")),
            P(("surf", "vol"), None),
            P(),
            P(),
            P(),
            P(("surf", "vol"), None),
        ),
        out_specs=(P(("surf", "vol"), None), P(("surf", "vol"), None)),
        check_vma=False,
    )
```

```python
import jax
import jax.numpy as jnp
from jax import lax
from jax.sharding import PartitionSpec as P

relax = 0.5


def contact(rows, mold_rows, stacked, joined, node_count):
    pair_rows = jnp.concatenate([rows[:, :node_count], mold_rows[:, :node_count]], axis=1)
    gap_jump = jnp.dot(pair_rows, stacked, preferred_element_type=jnp.float32)
    heat_flux = (
        rows[:, node_count:].astype(jnp.float32)
        * mold_rows[:, node_count:].astype(jnp.float32)
        * gap_jump
    ).astype(jnp.bfloat16)
    projected = jnp.dot(heat_flux, joined, preferred_element_type=jnp.float32)
    answer = jnp.concatenate([projected[:, :node_count], gap_jump], axis=1).astype(jnp.bfloat16)
    gained = projected[:, node_count:].astype(jnp.bfloat16)
    return (answer, gained)


def local(casting, owner, face_id, mold_faces, mortar_d, mortar_m, conduct, volume):
    seg_rows, row_width = casting.shape
    node_count = mortar_d.shape[0]
    face_rows = mold_faces.shape[0]
    surf_count = lax.axis_size("surf")
    vol_count = lax.axis_size("vol")
    devices = surf_count * vol_count
    capacity = 4 * seg_rows // devices
    slots = devices * capacity
    axes = ("surf", "vol")
    f32, bf16 = jnp.float32, jnp.bfloat16
    contract0 = (((0,), (0,)), ((), ()))

    target = owner[:, 0]
    hits = (target[:, None] == jnp.arange(devices, dtype=jnp.int32)[None, :]).astype(bf16)
    row_i = lax.broadcasted_iota(jnp.int32, (seg_rows, seg_rows), 0)
    row_j = lax.broadcasted_iota(jnp.int32, (seg_rows, seg_rows), 1)
    earlier = (row_j < row_i).astype(bf16)
    before = jnp.dot(earlier, hits, preferred_element_type=f32)
    position = jnp.sum(before * hits.astype(f32), axis=1).astype(jnp.int32)
    slot_index = target * capacity + position

    code = face_id + 1
    pos_hot = (position[:, None] == jnp.arange(capacity, dtype=jnp.int32)[None, :]).astype(bf16)
    hi = (code // 64).astype(bf16)[:, None]
    lo = (code % 64).astype(bf16)[:, None]
    id_hi = lax.dot_general(hits, pos_hot * hi, contract0, preferred_element_type=f32)
    id_lo = lax.dot_general(hits, pos_hot * lo, contract0, preferred_element_type=f32)
    id_count = 2 * capacity
    id_height = -(-id_count // row_width)
    id_flat = jnp.stack([id_hi, id_lo], axis=1).reshape(devices, id_count)
    id_flat = jnp.pad(id_flat, ((0, 0), (0, id_height * row_width - id_count)))
    id_rows = id_flat.reshape(devices, id_height, row_width)

    block = capacity + id_height
    send = jnp.zeros((devices, block, row_width), bf16).at[:, capacity:, :].set(id_rows.astype(bf16))
    send = send.reshape(devices * block, row_width).at[target * block + position].set(casting)
    send = send.reshape(devices, block, row_width)
    got = lax.all_to_all(send, axes, 0, 0, tiled=True)
    got_rows = got[:, :capacity, :].reshape(slots, row_width)
    got_code = got[:, capacity:, :].astype(f32).reshape(devices, id_height * row_width)
    got_code = got_code[:, :id_count].reshape(devices, 2, capacity)
    got_ids = (got_code[:, 0, :] * 64.0 + got_code[:, 1, :]).astype(jnp.int32).reshape(slots) - 1

    face_range = jnp.arange(face_rows, dtype=jnp.int32)
    selector = (got_ids[:, None] == face_range[None, :]).astype(bf16)
    mold_rows = jnp.dot(selector, mold_faces, preferred_element_type=f32).astype(bf16)

    stacked = jnp.concatenate([mortar_d.T, -mortar_m.T], axis=0)
    joined = jnp.concatenate([mortar_d, mortar_m], axis=1)
    answers, gained = contact(got_rows, mold_rows, stacked, joined, node_count)

    returned = lax.all_to_all(
        answers.reshape(devices, capacity, row_width), axes, 0, 0, tiled=True
    ).reshape(slots, row_width)
    totals = lax.dot_general(selector, gained, contract0, preferred_element_type=f32)
    quarter = face_rows // vol_count
    face_totals = totals.astype(bf16).reshape(vol_count, quarter * node_count // row_width, row_width)
    casting_out = jnp.take(returned, slot_index, axis=0)

    gathered = lax.all_gather(face_totals, "vol", axis=0)
    relaid = lax.dynamic_index_in_dim(gathered, lax.axis_index("vol"), axis=1, keepdims=False)
    heat = jnp.dot(volume, conduct, preferred_element_type=f32)
    placed = relaid.reshape(face_rows, node_count).astype(f32)
    inject = jnp.concatenate([placed, jnp.zeros((face_rows, node_count), f32)], axis=1)
    mold_out = (volume.astype(f32) + relax * (inject - heat)).astype(bf16)
    return (casting_out, mold_out)


def solution(mesh):
    return jax.shard_map(
        local,
        mesh=mesh,
        in_specs=(
            P(("surf", "vol"), None),
            P(("surf", "vol"), None),
            P(("surf", "vol")),
            P(("surf", "vol"), None),
            P(),
            P(),
            P(),
            P(("surf", "vol"), None),
        ),
        out_specs=(P(("surf", "vol"), None), P(("surf", "vol"), None)),
        check_vma=False,
    )
```

```python
import jax
import jax.numpy as jnp
from jax import lax
from jax.sharding import PartitionSpec as P

relax = 0.5


def contact(rows, mold_rows, stacked, joined, node_count):
    pair_rows = jnp.concatenate([rows[:, :node_count], mold_rows[:, :node_count]], axis=1)
    gap_jump = jnp.dot(pair_rows, stacked, preferred_element_type=jnp.float32)
    heat_flux = (
        rows[:, node_count:].astype(jnp.float32)
        * mold_rows[:, node_count:].astype(jnp.float32)
        * gap_jump
    ).astype(jnp.bfloat16)
    projected = jnp.dot(heat_flux, joined, preferred_element_type=jnp.float32)
    answer = jnp.concatenate([projected[:, :node_count], gap_jump], axis=1).astype(jnp.bfloat16)
    gained = projected[:, node_count:].astype(jnp.bfloat16)
    return (answer, gained)


def local(casting, owner, face_id, mold_faces, mortar_d, mortar_m, conduct, volume):
    seg_rows, row_width = casting.shape
    node_count = mortar_d.shape[0]
    face_rows = mold_faces.shape[0]
    surf_count = lax.axis_size("surf")
    vol_count = lax.axis_size("vol")
    devices = surf_count * vol_count
    capacity = 4 * seg_rows // devices
    slots = devices * capacity
    axes = ("surf", "vol")
    f32, bf16 = jnp.float32, jnp.bfloat16
    contract0 = (((0,), (0,)), ((), ()))

    target = owner[:, 0]
    hits = (target[:, None] == jnp.arange(devices, dtype=jnp.int32)[None, :]).astype(bf16)
    row_i = lax.broadcasted_iota(jnp.int32, (seg_rows, seg_rows), 0)
    row_j = lax.broadcasted_iota(jnp.int32, (seg_rows, seg_rows), 1)
    earlier = (row_j < row_i).astype(bf16)
    before = jnp.dot(earlier, hits, preferred_element_type=f32)
    position = jnp.sum(before * hits.astype(f32), axis=1).astype(jnp.int32)
    slot_index = target * capacity + position

    code = face_id + 1
    pos_hot = (position[:, None] == jnp.arange(capacity, dtype=jnp.int32)[None, :]).astype(bf16)
    hi = (code // 64).astype(bf16)[:, None]
    lo = (code % 64).astype(bf16)[:, None]
    id_hi = lax.dot_general(hits, pos_hot * hi, contract0, preferred_element_type=f32)
    id_lo = lax.dot_general(hits, pos_hot * lo, contract0, preferred_element_type=f32)
    id_count = 2 * capacity
    id_height = -(-id_count // row_width)
    id_flat = jnp.stack([id_hi, id_lo], axis=1).reshape(devices, id_count)
    id_flat = jnp.pad(id_flat, ((0, 0), (0, id_height * row_width - id_count)))
    id_rows = id_flat.reshape(devices, id_height, row_width)

    block = capacity + id_height
    send = jnp.zeros((devices, block, row_width), bf16).at[:, capacity:, :].set(id_rows.astype(bf16))
    send = send.reshape(devices * block, row_width).at[target * block + position].set(casting)
    send = send.reshape(devices, block, row_width)
    got = lax.all_to_all(send, axes, 0, 0, tiled=True)
    got_rows = got[:, :capacity, :].reshape(slots, row_width)
    got_code = got[:, capacity:, :].astype(f32).reshape(devices, id_height * row_width)
    got_code = got_code[:, :id_count].reshape(devices, 2, capacity)
    got_ids = (got_code[:, 0, :] * 64.0 + got_code[:, 1, :]).astype(jnp.int32).reshape(slots) - 1

    face_range = jnp.arange(face_rows, dtype=jnp.int32)
    selector = (got_ids[:, None] == face_range[None, :]).astype(bf16)
    mold_rows = jnp.take(mold_faces, jnp.maximum(got_ids, 0), axis=0)

    stacked = jnp.concatenate([mortar_d.T, -mortar_m.T], axis=0)
    joined = jnp.concatenate([mortar_d, mortar_m], axis=1)
    answers, gained = contact(got_rows, mold_rows, stacked, joined, node_count)

    returned = lax.all_to_all(
        answers.reshape(devices, capacity, row_width), axes, 0, 0, tiled=True
    ).reshape(slots, row_width)
    totals = lax.dot_general(selector, gained, contract0, preferred_element_type=f32)
    quarter = face_rows // vol_count
    face_totals = totals.astype(bf16).reshape(vol_count, quarter * node_count // row_width, row_width)
    face_totals, returned = lax.optimization_barrier((face_totals, returned))
    casting_out = jnp.take(returned, slot_index, axis=0)

    relaid = lax.all_to_all(
        face_totals,
        "vol",
        split_axis=0,
        concat_axis=0,
        tiled=True,
    )
    heat = jnp.dot(volume, conduct, preferred_element_type=f32)
    placed = relaid.reshape(face_rows, node_count).astype(f32)
    inject = jnp.concatenate([placed, jnp.zeros((face_rows, node_count), f32)], axis=1)
    mold_out = (volume.astype(f32) + relax * (inject - heat)).astype(bf16)
    return (casting_out, mold_out)


def solution(mesh):
    return jax.shard_map(
        local,
        mesh=mesh,
        in_specs=(
            P(("surf", "vol"), None),
            P(("surf", "vol"), None),
            P(("surf", "vol")),
            P(("surf", "vol"), None),
            P(),
            P(),
            P(),
            P(("surf", "vol"), None),
        ),
        out_specs=(P(("surf", "vol"), None), P(("surf", "vol"), None)),
        check_vma=False,
    )
```

```python
import jax
import jax.numpy as jnp
from jax import lax
from jax.sharding import PartitionSpec as P

relax = 0.5


def contact(rows, mold_rows, stacked, joined, node_count):
    pair_rows = jnp.concatenate([rows[:, :node_count], mold_rows[:, :node_count]], axis=1)
    gap_jump = jnp.dot(pair_rows, stacked, preferred_element_type=jnp.float32)
    heat_flux = (
        rows[:, node_count:].astype(jnp.float32)
        * mold_rows[:, node_count:].astype(jnp.float32)
        * gap_jump
    ).astype(jnp.bfloat16)
    projected = jnp.dot(heat_flux, joined, preferred_element_type=jnp.float32)
    answer = jnp.concatenate([projected[:, :node_count], gap_jump], axis=1).astype(jnp.bfloat16)
    gained = projected[:, node_count:].astype(jnp.bfloat16)
    return (answer, gained)


def local(casting, owner, face_id, mold_faces, mortar_d, mortar_m, conduct, volume):
    seg_rows, row_width = casting.shape
    node_count = mortar_d.shape[0]
    face_rows = mold_faces.shape[0]
    surf_count = lax.axis_size("surf")
    vol_count = lax.axis_size("vol")
    devices = surf_count * vol_count
    capacity = 4 * seg_rows // devices
    slots = devices * capacity
    axes = ("surf", "vol")
    f32, bf16 = jnp.float32, jnp.bfloat16
    contract0 = (((0,), (0,)), ((), ()))

    target = owner[:, 0]
    hits = (target[:, None] == jnp.arange(devices, dtype=jnp.int32)[None, :]).astype(bf16)
    row_i = lax.broadcasted_iota(jnp.int32, (seg_rows, seg_rows), 0)
    row_j = lax.broadcasted_iota(jnp.int32, (seg_rows, seg_rows), 1)
    earlier = (row_j < row_i).astype(bf16)
    before = jnp.dot(earlier, hits, preferred_element_type=f32)
    position = jnp.sum(before * hits.astype(f32), axis=1).astype(jnp.int32)
    slot_index = target * capacity + position

    code = face_id + 1
    pos_hot = (position[:, None] == jnp.arange(capacity, dtype=jnp.int32)[None, :]).astype(bf16)
    hi = (code // 64).astype(bf16)[:, None]
    lo = (code % 64).astype(bf16)[:, None]
    id_hi = lax.dot_general(hits, pos_hot * hi, contract0, preferred_element_type=f32)
    id_lo = lax.dot_general(hits, pos_hot * lo, contract0, preferred_element_type=f32)
    id_count = 2 * capacity
    id_height = -(-id_count // row_width)
    id_flat = jnp.stack([id_hi, id_lo], axis=1).reshape(devices, id_count)
    id_flat = jnp.pad(id_flat, ((0, 0), (0, id_height * row_width - id_count)))
    id_rows = id_flat.reshape(devices, id_height, row_width)

    block = capacity + id_height
    send = jnp.zeros((devices, block, row_width), bf16).at[:, capacity:, :].set(id_rows.astype(bf16))
    send = send.reshape(devices * block, row_width).at[target * block + position].set(casting)
    send = send.reshape(devices, block, row_width)
    got = lax.all_to_all(send, axes, 0, 0, tiled=True)
    got_rows = got[:, :capacity, :].reshape(slots, row_width)
    got_code = got[:, capacity:, :].astype(f32).reshape(devices, id_height * row_width)
    got_code = got_code[:, :id_count].reshape(devices, 2, capacity)
    got_ids = (got_code[:, 0, :] * 64.0 + got_code[:, 1, :]).astype(jnp.int32).reshape(slots) - 1

    face_range = jnp.arange(face_rows, dtype=jnp.int32)
    selector = (got_ids[:, None] == face_range[None, :]).astype(bf16)
    mold_rows = jnp.dot(selector, mold_faces, preferred_element_type=f32).astype(bf16)

    zero = jnp.zeros((node_count, node_count), bf16)
    wc = jnp.block([[zero, mortar_d.T], [zero, zero]])
    wm = jnp.block([[zero, -mortar_m.T], [zero, zero]])
    wj = jnp.block([[zero, zero], [mortar_d, mortar_m]])
    gap = jnp.dot(got_rows, wc, preferred_element_type=f32) + jnp.dot(
        mold_rows, wm, preferred_element_type=f32
    )
    flux = (got_rows.astype(f32) * mold_rows.astype(f32) * gap).astype(bf16)
    projected = jnp.dot(flux, wj, preferred_element_type=f32)
    lane = lax.broadcasted_iota(jnp.int32, (slots, row_width), 1)
    answers = jnp.where(lane < node_count, projected, gap).astype(bf16)
    gained = projected[:, node_count:].astype(bf16)

    returned = lax.all_to_all(
        answers.reshape(devices, capacity, row_width), axes, 0, 0, tiled=True
    ).reshape(slots, row_width)
    totals = lax.dot_general(selector, gained, contract0, preferred_element_type=f32)
    quarter = face_rows // vol_count
    face_totals = totals.astype(bf16).reshape(vol_count, quarter * node_count // row_width, row_width)
    face_totals, returned = lax.optimization_barrier((face_totals, returned))
    casting_out = jnp.take(returned, slot_index, axis=0)

    relaid = lax.all_to_all(
        face_totals,
        "vol",
        split_axis=0,
        concat_axis=0,
        tiled=True,
    )
    heat = jnp.dot(volume, conduct, preferred_element_type=f32)
    placed = relaid.reshape(face_rows, node_count).astype(f32)
    inject = jnp.concatenate([placed, jnp.zeros((face_rows, node_count), f32)], axis=1)
    mold_out = (volume.astype(f32) + relax * (inject - heat)).astype(bf16)
    return (casting_out, mold_out)


def solution(mesh):
    return jax.shard_map(
        local,
        mesh=mesh,
        in_specs=(
            P(("surf", "vol"), None),
            P(("surf", "vol"), None),
            P(("surf", "vol")),
            P(("surf", "vol"), None),
            P(),
            P(),
            P(),
            P(("surf", "vol"), None),
        ),
        out_specs=(P(("surf", "vol"), None), P(("surf", "vol"), None)),
        check_vma=False,
    )
```

```python
import jax
import jax.numpy as jnp
from jax import lax
from jax.sharding import PartitionSpec as P

relax = 0.5


def contact(rows, mold_rows, stacked, joined, node_count):
    pair_rows = jnp.concatenate([rows[:, :node_count], mold_rows[:, :node_count]], axis=1)
    gap_jump = jnp.dot(pair_rows, stacked, preferred_element_type=jnp.float32)
    heat_flux = (
        rows[:, node_count:].astype(jnp.float32)
        * mold_rows[:, node_count:].astype(jnp.float32)
        * gap_jump
    ).astype(jnp.bfloat16)
    projected = jnp.dot(heat_flux, joined, preferred_element_type=jnp.float32)
    answer = jnp.concatenate([projected[:, :node_count], gap_jump], axis=1).astype(jnp.bfloat16)
    gained = projected[:, node_count:].astype(jnp.bfloat16)
    return (answer, gained)


def local(casting, owner, face_id, mold_faces, mortar_d, mortar_m, conduct, volume):
    seg_rows, row_width = casting.shape
    node_count = mortar_d.shape[0]
    face_rows = mold_faces.shape[0]
    surf_count = lax.axis_size("surf")
    vol_count = lax.axis_size("vol")
    devices = surf_count * vol_count
    capacity = 4 * seg_rows // devices
    slots = devices * capacity
    axes = ("surf", "vol")
    f32, bf16 = jnp.float32, jnp.bfloat16
    contract0 = (((0,), (0,)), ((), ()))

    target = owner[:, 0]
    hits = (target[:, None] == jnp.arange(devices, dtype=jnp.int32)[None, :]).astype(bf16)
    row_i = lax.broadcasted_iota(jnp.int32, (seg_rows, seg_rows), 0)
    row_j = lax.broadcasted_iota(jnp.int32, (seg_rows, seg_rows), 1)
    earlier = (row_j < row_i).astype(bf16)
    before = jnp.dot(earlier, hits, preferred_element_type=f32)
    position = jnp.sum(before * hits.astype(f32), axis=1).astype(jnp.int32)
    slot_index = target * capacity + position

    code = face_id + 1
    pos_hot = (position[:, None] == jnp.arange(capacity, dtype=jnp.int32)[None, :]).astype(bf16)
    hi = (code // 64).astype(bf16)[:, None]
    lo = (code % 64).astype(bf16)[:, None]
    id_count = 2 * capacity
    id_height = -(-id_count // row_width)
    codes = jnp.concatenate([pos_hot * hi, pos_hot * lo], axis=1)
    id_flat = lax.dot_general(hits, codes, contract0, preferred_element_type=f32)
    id_flat = jnp.pad(id_flat, ((0, 0), (0, id_height * row_width - id_count)))
    id_rows = id_flat.reshape(devices, id_height, row_width)

    send_rows = jnp.zeros((slots, row_width), bf16).at[slot_index].set(casting)
    send = jnp.concatenate(
        [send_rows.reshape(devices, capacity, row_width), id_rows.astype(bf16)], axis=1
    )
    got = lax.all_to_all(send, axes, 0, 0, tiled=True)
    got_rows = got[:, :capacity, :].reshape(slots, row_width)
    got_code = got[:, capacity:, :].astype(f32).reshape(devices, id_height * row_width)
    got_code = got_code[:, :id_count].reshape(devices, 2, capacity)
    got_ids = (got_code[:, 0, :] * 64.0 + got_code[:, 1, :]).astype(jnp.int32).reshape(slots) - 1

    face_range = jnp.arange(face_rows, dtype=jnp.int32)
    selector = (got_ids[:, None] == face_range[None, :]).astype(bf16)
    mold_rows = jnp.dot(selector, mold_faces, preferred_element_type=f32).astype(bf16)

    zero = jnp.zeros((node_count, node_count), bf16)
    wc = jnp.block([[zero, mortar_d.T], [zero, zero]])
    wm = jnp.block([[zero, -mortar_m.T], [zero, zero]])
    wj = jnp.block([[zero, zero], [mortar_d, mortar_m]])
    gap = jnp.dot(got_rows, wc, preferred_element_type=f32) + jnp.dot(
        mold_rows, wm, preferred_element_type=f32
    )
    flux = (got_rows.astype(f32) * mold_rows.astype(f32) * gap).astype(bf16)
    projected = jnp.dot(flux, wj, preferred_element_type=f32)
    lane = lax.broadcasted_iota(jnp.int32, (slots, row_width), 1)
    answers = jnp.where(lane < node_count, projected, gap).astype(bf16)
    gained = projected[:, node_count:].astype(bf16)

    returned = lax.all_to_all(
        answers.reshape(devices, capacity, row_width), axes, 0, 0, tiled=True
    ).reshape(slots, row_width)
    totals = lax.dot_general(selector, gained, contract0, preferred_element_type=f32)
    quarter = face_rows // vol_count
    face_totals = totals.astype(bf16).reshape(vol_count, quarter * node_count // row_width, row_width)
    face_totals, returned = lax.optimization_barrier((face_totals, returned))
    casting_out = jnp.take(returned, slot_index, axis=0)

    relaid = lax.all_to_all(
        face_totals,
        "vol",
        split_axis=0,
        concat_axis=0,
        tiled=True,
    )
    heat = jnp.dot(volume, conduct, preferred_element_type=f32)
    placed = relaid.reshape(face_rows, node_count).astype(f32)
    inject = jnp.concatenate([placed, jnp.zeros((face_rows, node_count), f32)], axis=1)
    mold_out = (volume.astype(f32) + relax * (inject - heat)).astype(bf16)
    return (casting_out, mold_out)


def solution(mesh):
    return jax.shard_map(
        local,
        mesh=mesh,
        in_specs=(
            P(("surf", "vol"), None),
            P(("surf", "vol"), None),
            P(("surf", "vol")),
            P(("surf", "vol"), None),
            P(),
            P(),
            P(),
            P(("surf", "vol"), None),
        ),
        out_specs=(P(("surf", "vol"), None), P(("surf", "vol"), None)),
        check_vma=False,
    )
```

```python
import jax
import jax.numpy as jnp
from jax import lax
from jax.sharding import PartitionSpec as P

relax = 0.5


def contact(rows, mold_rows, stacked, joined, node_count):
    pair_rows = jnp.concatenate([rows[:, :node_count], mold_rows[:, :node_count]], axis=1)
    gap_jump = jnp.dot(pair_rows, stacked, preferred_element_type=jnp.float32)
    heat_flux = (
        rows[:, node_count:].astype(jnp.float32)
        * mold_rows[:, node_count:].astype(jnp.float32)
        * gap_jump
    ).astype(jnp.bfloat16)
    projected = jnp.dot(heat_flux, joined, preferred_element_type=jnp.float32)
    answer = jnp.concatenate([projected[:, :node_count], gap_jump], axis=1).astype(jnp.bfloat16)
    gained = projected[:, node_count:].astype(jnp.bfloat16)
    return (answer, gained)


def local(casting, owner, face_id, mold_faces, mortar_d, mortar_m, conduct, volume):
    seg_rows, row_width = casting.shape
    node_count = mortar_d.shape[0]
    face_rows = mold_faces.shape[0]
    surf_count = lax.axis_size("surf")
    vol_count = lax.axis_size("vol")
    devices = surf_count * vol_count
    capacity = 4 * seg_rows // devices
    slots = devices * capacity
    axes = ("surf", "vol")
    f32, bf16 = jnp.float32, jnp.bfloat16
    contract0 = (((0,), (0,)), ((), ()))

    target = owner[:, 0]
    hits = (target[:, None] == jnp.arange(devices, dtype=jnp.int32)[None, :]).astype(bf16)
    row_i = lax.broadcasted_iota(jnp.int32, (seg_rows, seg_rows), 0)
    row_j = lax.broadcasted_iota(jnp.int32, (seg_rows, seg_rows), 1)
    earlier = (row_j < row_i).astype(bf16)
    before = jnp.dot(earlier, hits, preferred_element_type=f32)
    position = jnp.sum(before * hits.astype(f32), axis=1).astype(jnp.int32)
    slot_index = target * capacity + position

    code = face_id + 1
    pos_hot = (position[:, None] == jnp.arange(capacity, dtype=jnp.int32)[None, :]).astype(bf16)
    hi = (code // 64).astype(bf16)[:, None]
    lo = (code % 64).astype(bf16)[:, None]
    id_count = 2 * capacity
    id_height = -(-id_count // row_width)
    codes = jnp.concatenate([pos_hot * hi, pos_hot * lo], axis=1)
    id_flat = lax.dot_general(hits, codes, contract0, preferred_element_type=f32)
    id_flat = jnp.pad(id_flat, ((0, 0), (0, id_height * row_width - id_count)))
    id_rows = id_flat.reshape(devices, id_height, row_width)

    send_rows = jnp.zeros((slots, row_width), bf16).at[slot_index].set(casting)
    send = jnp.concatenate(
        [send_rows.reshape(devices, capacity, row_width), id_rows.astype(bf16)], axis=1
    )
    got = lax.all_to_all(send, axes, 0, 0, tiled=True)
    got_rows = got[:, :capacity, :].reshape(slots, row_width)
    got_code = got[:, capacity:, :].astype(f32).reshape(devices, id_height * row_width)
    got_code = got_code[:, :id_count].reshape(devices, 2, capacity)
    got_ids = (got_code[:, 0, :] * 64.0 + got_code[:, 1, :]).astype(jnp.int32).reshape(slots) - 1

    face_range = jnp.arange(face_rows, dtype=jnp.int32)
    selector = (got_ids[:, None] == face_range[None, :]).astype(bf16)
    mold_rows = jnp.dot(selector, mold_faces, preferred_element_type=f32).astype(bf16)

    zero = jnp.zeros((node_count, node_count), bf16)
    wc = jnp.block([[zero, mortar_d.T], [zero, zero]])
    wm = jnp.block([[zero, -mortar_m.T], [zero, zero]])
    wj = jnp.block([[zero, zero], [mortar_d, mortar_m]])
    gap = jnp.dot(got_rows, wc, preferred_element_type=f32) + jnp.dot(
        mold_rows, wm, preferred_element_type=f32
    )
    flux = (got_rows.astype(f32) * mold_rows.astype(f32) * gap).astype(bf16)
    projected = jnp.dot(flux, wj, preferred_element_type=f32)
    lane = lax.broadcasted_iota(jnp.int32, (slots, row_width), 1)
    answers = jnp.where(lane < node_count, projected, gap).astype(bf16)
    gained = projected[:, node_count:].astype(bf16)

    returned = lax.all_to_all(
        answers.reshape(devices, capacity, row_width), axes, 0, 0, tiled=True
    ).reshape(slots, row_width)
    totals = lax.dot_general(selector, gained, contract0, preferred_element_type=f32)
    quarter = face_rows // vol_count
    face_totals = totals.astype(bf16).reshape(vol_count, quarter * node_count // row_width, row_width)
    face_totals, returned = lax.optimization_barrier((face_totals, returned))
    casting_out = jnp.take(returned, slot_index, axis=0, mode="clip")

    relaid = lax.all_to_all(
        face_totals,
        "vol",
        split_axis=0,
        concat_axis=0,
        tiled=True,
    )
    heat = jnp.dot(volume, conduct, preferred_element_type=f32)
    settled = volume.astype(f32) - relax * heat
    settled, relaid = lax.optimization_barrier((settled, relaid))
    placed = relaid.reshape(face_rows, node_count).astype(f32)
    inject = jnp.concatenate([placed, jnp.zeros((face_rows, node_count), f32)], axis=1)
    mold_out = (settled + relax * inject).astype(bf16)
    return (casting_out, mold_out)


def solution(mesh):
    return jax.shard_map(
        local,
        mesh=mesh,
        in_specs=(
            P(("surf", "vol"), None),
            P(("surf", "vol"), None),
            P(("surf", "vol")),
            P(("surf", "vol"), None),
            P(),
            P(),
            P(),
            P(("surf", "vol"), None),
        ),
        out_specs=(P(("surf", "vol"), None), P(("surf", "vol"), None)),
        check_vma=False,
    )
```

```python
import math

import jax
import jax.numpy as jnp
from jax import lax
from jax.sharding import PartitionSpec as P

relax = 0.5


def contact(rows, mold_rows, stacked, joined, node_count):
    pair_rows = jnp.concatenate([rows[:, :node_count], mold_rows[:, :node_count]], axis=1)
    gap_jump = jnp.dot(pair_rows, stacked, preferred_element_type=jnp.float32)
    heat_flux = (
        rows[:, node_count:].astype(jnp.float32)
        * mold_rows[:, node_count:].astype(jnp.float32)
        * gap_jump
    ).astype(jnp.bfloat16)
    projected = jnp.dot(heat_flux, joined, preferred_element_type=jnp.float32)
    answer = jnp.concatenate([projected[:, :node_count], gap_jump], axis=1).astype(jnp.bfloat16)
    gained = projected[:, node_count:].astype(jnp.bfloat16)
    return (answer, gained)


def local(casting, owner, face_id, mold_faces, mortar_d, mortar_m, conduct, volume):
    seg_rows, row_width = casting.shape
    node_count = mortar_d.shape[0]
    face_rows = mold_faces.shape[0]
    surf_count = lax.axis_size("surf")
    vol_count = lax.axis_size("vol")
    devices = surf_count * vol_count
    capacity = 4 * seg_rows // devices
    slots = devices * capacity
    axes = ("surf", "vol")
    f32, bf16 = jnp.float32, jnp.bfloat16
    contract0 = (((0,), (0,)), ((), ()))

    target = owner[:, 0]
    hits = (target[:, None] == jnp.arange(devices, dtype=jnp.int32)[None, :]).astype(bf16)
    span = math.gcd(seg_rows, 128)
    spans = seg_rows // span
    row_i = lax.broadcasted_iota(jnp.int32, (span, span), 0)
    row_j = lax.broadcasted_iota(jnp.int32, (span, span), 1)
    earlier = (row_j < row_i).astype(bf16)
    hit_blocks = hits.reshape(spans, span, devices)
    within = jnp.einsum("ij,bjd->bid", earlier, hit_blocks, preferred_element_type=f32)
    block_totals = jnp.sum(hit_blocks.astype(f32), axis=1).astype(bf16)
    blk_i = lax.broadcasted_iota(jnp.int32, (spans, spans), 0)
    blk_j = lax.broadcasted_iota(jnp.int32, (spans, spans), 1)
    prior = jnp.dot((blk_j < blk_i).astype(bf16), block_totals, preferred_element_type=f32)
    before = within + prior[:, None, :]
    position = jnp.sum(before * hit_blocks.astype(f32), axis=2).reshape(seg_rows).astype(jnp.int32)
    slot_index = target * capacity + position

    code = face_id + 1
    pos_hot = (position[:, None] == jnp.arange(capacity, dtype=jnp.int32)[None, :]).astype(bf16)
    hi = (code // 64).astype(bf16)[:, None]
    lo = (code % 64).astype(bf16)[:, None]
    id_count = 2 * capacity
    id_height = -(-id_count // row_width)
    codes = jnp.concatenate([pos_hot * hi, pos_hot * lo], axis=1)
    id_flat = lax.dot_general(hits, codes, contract0, preferred_element_type=f32)
    id_flat = jnp.pad(id_flat, ((0, 0), (0, id_height * row_width - id_count)))
    id_rows = id_flat.reshape(devices, id_height, row_width)

    send_rows = jnp.zeros((slots, row_width), bf16).at[slot_index].set(casting)
    send = jnp.concatenate(
        [send_rows.reshape(devices, capacity, row_width), id_rows.astype(bf16)], axis=1
    )
    got = lax.all_to_all(send, axes, 0, 0, tiled=True)
    got_rows = got[:, :capacity, :].reshape(slots, row_width)
    got_code = got[:, capacity:, :].astype(f32).reshape(devices, id_height * row_width)
    got_code = got_code[:, :id_count].reshape(devices, 2, capacity)
    got_ids = (got_code[:, 0, :] * 64.0 + got_code[:, 1, :]).astype(jnp.int32).reshape(slots) - 1

    face_range = jnp.arange(face_rows, dtype=jnp.int32)
    selector = (got_ids[:, None] == face_range[None, :]).astype(bf16)
    mold_rows = jnp.dot(selector, mold_faces, preferred_element_type=f32).astype(bf16)

    zero = jnp.zeros((node_count, node_count), bf16)
    wc = jnp.block([[zero, mortar_d.T], [zero, zero]])
    wm = jnp.block([[zero, -mortar_m.T], [zero, zero]])
    wj = jnp.block([[zero, zero], [mortar_d, mortar_m]])
    gap = jnp.dot(got_rows, wc, preferred_element_type=f32) + jnp.dot(
        mold_rows, wm, preferred_element_type=f32
    )
    flux = (got_rows.astype(f32) * mold_rows.astype(f32) * gap).astype(bf16)
    projected = jnp.dot(flux, wj, preferred_element_type=f32)
    lane = lax.broadcasted_iota(jnp.int32, (slots, row_width), 1)
    answers = jnp.where(lane < node_count, projected, gap).astype(bf16)
    gained = projected[:, node_count:].astype(bf16)

    returned = lax.all_to_all(
        answers.reshape(devices, capacity, row_width), axes, 0, 0, tiled=True
    ).reshape(slots, row_width)
    totals = lax.dot_general(selector, gained, contract0, preferred_element_type=f32)
    quarter = face_rows // vol_count
    face_totals = totals.astype(bf16).reshape(vol_count, quarter * node_count // row_width, row_width)
    face_totals, returned = lax.optimization_barrier((face_totals, returned))
    casting_out = jnp.take(returned, slot_index, axis=0, mode="clip")

    relaid = lax.all_to_all(
        face_totals,
        "vol",
        split_axis=0,
        concat_axis=0,
        tiled=True,
    )
    heat = jnp.dot(volume, conduct, preferred_element_type=f32)
    settled = volume.astype(f32) - relax * heat
    settled, relaid = lax.optimization_barrier((settled, relaid))
    placed = relaid.reshape(face_rows, node_count).astype(f32)
    inject = jnp.concatenate([placed, jnp.zeros((face_rows, node_count), f32)], axis=1)
    mold_out = (settled + relax * inject).astype(bf16)
    return (casting_out, mold_out)


def solution(mesh):
    return jax.shard_map(
        local,
        mesh=mesh,
        in_specs=(
            P(("surf", "vol"), None),
            P(("surf", "vol"), None),
            P(("surf", "vol")),
            P(("surf", "vol"), None),
            P(),
            P(),
            P(),
            P(("surf", "vol"), None),
        ),
        out_specs=(P(("surf", "vol"), None), P(("surf", "vol"), None)),
        check_vma=False,
    )
```

```python
import jax
import jax.numpy as jnp
from jax import lax
from jax.sharding import PartitionSpec as P

relax = 0.5


def contact(rows, mold_rows, stacked, joined, node_count):
    pair_rows = jnp.concatenate([rows[:, :node_count], mold_rows[:, :node_count]], axis=1)
    gap_jump = jnp.dot(pair_rows, stacked, preferred_element_type=jnp.float32)
    heat_flux = (
        rows[:, node_count:].astype(jnp.float32)
        * mold_rows[:, node_count:].astype(jnp.float32)
        * gap_jump
    ).astype(jnp.bfloat16)
    projected = jnp.dot(heat_flux, joined, preferred_element_type=jnp.float32)
    answer = jnp.concatenate([projected[:, :node_count], gap_jump], axis=1).astype(jnp.bfloat16)
    gained = projected[:, node_count:].astype(jnp.bfloat16)
    return (answer, gained)


def local(casting, owner, face_id, mold_faces, mortar_d, mortar_m, conduct, volume):
    seg_rows, row_width = casting.shape
    node_count = mortar_d.shape[0]
    face_rows = mold_faces.shape[0]
    surf_count = lax.axis_size("surf")
    vol_count = lax.axis_size("vol")
    devices = surf_count * vol_count
    capacity = 4 * seg_rows // devices
    slots = devices * capacity
    axes = ("surf", "vol")
    f32, bf16 = jnp.float32, jnp.bfloat16
    contract0 = (((0,), (0,)), ((), ()))

    target = owner[:, 0]
    hits = (target[:, None] == jnp.arange(devices, dtype=jnp.int32)[None, :]).astype(bf16)
    row_i = lax.broadcasted_iota(jnp.int32, (seg_rows, seg_rows), 0)
    row_j = lax.broadcasted_iota(jnp.int32, (seg_rows, seg_rows), 1)
    earlier = (row_j < row_i).astype(bf16)
    before = jnp.dot(earlier, hits, preferred_element_type=f32)
    position = jnp.sum(before * hits.astype(f32), axis=1).astype(jnp.int32)
    slot_index = target * capacity + position

    code = face_id + 1
    pos_hot = (position[:, None] == jnp.arange(capacity, dtype=jnp.int32)[None, :]).astype(bf16)
    hi = (code // 64).astype(bf16)[:, None]
    lo = (code % 64).astype(bf16)[:, None]
    id_count = 2 * capacity
    id_height = -(-id_count // row_width)
    codes = jnp.concatenate([pos_hot * hi, pos_hot * lo], axis=1)
    id_flat = lax.dot_general(hits, codes, contract0, preferred_element_type=f32)
    id_flat = jnp.pad(id_flat, ((0, 0), (0, id_height * row_width - id_count)))
    id_rows = id_flat.reshape(devices, id_height, row_width)

    send_rows = jnp.zeros((slots, row_width), bf16).at[slot_index].set(casting)
    send = jnp.concatenate(
        [send_rows.reshape(devices, capacity, row_width), id_rows.astype(bf16)], axis=1
    )
    got = lax.all_to_all(send, axes, 0, 0, tiled=True)
    got_rows = got[:, :capacity, :].reshape(slots, row_width)
    got_code = got[:, capacity:, :].astype(f32).reshape(devices, id_height * row_width)
    got_code = got_code[:, :id_count].reshape(devices, 2, capacity)
    got_ids = (got_code[:, 0, :] * 64.0 + got_code[:, 1, :]).astype(jnp.int32).reshape(slots) - 1

    face_range = jnp.arange(face_rows, dtype=jnp.int32)
    selector = (got_ids[:, None] == face_range[None, :]).astype(bf16)
    mold_rows = jnp.dot(selector, mold_faces, preferred_element_type=f32).astype(bf16)

    zero = jnp.zeros((node_count, node_count), bf16)
    wc = jnp.block([[zero, mortar_d.T], [zero, zero]])
    wm = jnp.block([[zero, -mortar_m.T], [zero, zero]])
    wb = jnp.block([[zero, zero], [mortar_d, zero]])
    wg = jnp.concatenate([zero, mortar_m], axis=0)
    gap = jnp.dot(got_rows, wc, preferred_element_type=f32) + jnp.dot(
        mold_rows, wm, preferred_element_type=f32
    )
    flux = (got_rows.astype(f32) * mold_rows.astype(f32) * gap).astype(bf16)
    answers = (jnp.dot(flux, wb, preferred_element_type=f32) + gap).astype(bf16)
    gained = jnp.dot(flux, wg, preferred_element_type=f32).astype(bf16)

    returned = lax.all_to_all(
        answers.reshape(devices, capacity, row_width), axes, 0, 0, tiled=True
    ).reshape(slots, row_width)
    totals = lax.dot_general(selector, gained, contract0, preferred_element_type=f32)
    quarter = face_rows // vol_count
    face_totals = totals.astype(bf16).reshape(vol_count, quarter * node_count // row_width, row_width)
    face_totals, returned = lax.optimization_barrier((face_totals, returned))
    casting_out = jnp.take(returned, slot_index, axis=0, mode="clip")

    relaid = lax.all_to_all(
        face_totals,
        "vol",
        split_axis=0,
        concat_axis=0,
        tiled=True,
    )
    heat = jnp.dot(volume, conduct, preferred_element_type=f32)
    settled = volume.astype(f32) - relax * heat
    settled, relaid = lax.optimization_barrier((settled, relaid))
    placed = relaid.reshape(face_rows, node_count).astype(f32)
    inject = jnp.concatenate([placed, jnp.zeros((face_rows, node_count), f32)], axis=1)
    mold_out = (settled + relax * inject).astype(bf16)
    return (casting_out, mold_out)


def solution(mesh):
    return jax.shard_map(
        local,
        mesh=mesh,
        in_specs=(
            P(("surf", "vol"), None),
            P(("surf", "vol"), None),
            P(("surf", "vol")),
            P(("surf", "vol"), None),
            P(),
            P(),
            P(),
            P(("surf", "vol"), None),
        ),
        out_specs=(P(("surf", "vol"), None), P(("surf", "vol"), None)),
        check_vma=False,
    )
```

```python
import jax
import jax.numpy as jnp
from jax import lax
from jax.sharding import PartitionSpec as P

relax = 0.5


def contact(rows, mold_rows, stacked, joined, node_count):
    pair_rows = jnp.concatenate([rows[:, :node_count], mold_rows[:, :node_count]], axis=1)
    gap_jump = jnp.dot(pair_rows, stacked, preferred_element_type=jnp.float32)
    heat_flux = (
        rows[:, node_count:].astype(jnp.float32)
        * mold_rows[:, node_count:].astype(jnp.float32)
        * gap_jump
    ).astype(jnp.bfloat16)
    projected = jnp.dot(heat_flux, joined, preferred_element_type=jnp.float32)
    answer = jnp.concatenate([projected[:, :node_count], gap_jump], axis=1).astype(jnp.bfloat16)
    gained = projected[:, node_count:].astype(jnp.bfloat16)
    return (answer, gained)


def local(casting, owner, face_id, mold_faces, mortar_d, mortar_m, conduct, volume):
    seg_rows, row_width = casting.shape
    node_count = mortar_d.shape[0]
    face_rows = mold_faces.shape[0]
    surf_count = lax.axis_size("surf")
    vol_count = lax.axis_size("vol")
    devices = surf_count * vol_count
    capacity = 4 * seg_rows // devices
    slots = devices * capacity
    axes = ("surf", "vol")
    f32, bf16 = jnp.float32, jnp.bfloat16
    contract0 = (((0,), (0,)), ((), ()))

    target = owner[:, 0]
    hits = (target[:, None] == jnp.arange(devices, dtype=jnp.int32)[None, :]).astype(bf16)
    row_i = lax.broadcasted_iota(jnp.int32, (seg_rows, seg_rows), 0)
    row_j = lax.broadcasted_iota(jnp.int32, (seg_rows, seg_rows), 1)
    earlier = (row_j < row_i).astype(bf16)
    before = jnp.dot(earlier, hits, preferred_element_type=f32)
    position = jnp.sum(before * hits.astype(f32), axis=1).astype(jnp.int32)
    slot_index = target * capacity + position

    code = face_id + 1
    pos_hot = (position[:, None] == jnp.arange(capacity, dtype=jnp.int32)[None, :]).astype(bf16)
    hi = (code // 64).astype(bf16)[:, None]
    lo = (code % 64).astype(bf16)[:, None]
    id_count = 2 * capacity
    id_height = -(-id_count // row_width)
    codes = jnp.concatenate([pos_hot * hi, pos_hot * lo], axis=1)
    id_flat = lax.dot_general(hits, codes, contract0, preferred_element_type=f32)
    id_flat = jnp.pad(id_flat, ((0, 0), (0, id_height * row_width - id_count)))
    id_rows = id_flat.reshape(devices, id_height, row_width)

    slot_hot = (lax.broadcasted_iota(jnp.int32, (slots, seg_rows), 0) == slot_index[None, :]).astype(bf16)
    send_rows = jnp.dot(slot_hot, casting, preferred_element_type=f32).astype(bf16)
    send = jnp.concatenate(
        [send_rows.reshape(devices, capacity, row_width), id_rows.astype(bf16)], axis=1
    )
    got = lax.all_to_all(send, axes, 0, 0, tiled=True)
    got_rows = got[:, :capacity, :].reshape(slots, row_width)
    got_code = got[:, capacity:, :].astype(f32).reshape(devices, id_height * row_width)
    got_code = got_code[:, :id_count].reshape(devices, 2, capacity)
    got_ids = (got_code[:, 0, :] * 64.0 + got_code[:, 1, :]).astype(jnp.int32).reshape(slots) - 1

    face_range = jnp.arange(face_rows, dtype=jnp.int32)
    selector = (got_ids[:, None] == face_range[None, :]).astype(bf16)
    mold_rows = jnp.dot(selector, mold_faces, preferred_element_type=f32).astype(bf16)

    zero = jnp.zeros((node_count, node_count), bf16)
    wc = jnp.block([[zero, mortar_d.T], [zero, zero]])
    wm = jnp.block([[zero, -mortar_m.T], [zero, zero]])
    wj = jnp.block([[zero, zero], [mortar_d, mortar_m]])
    gap = jnp.dot(got_rows, wc, preferred_element_type=f32) + jnp.dot(
        mold_rows, wm, preferred_element_type=f32
    )
    flux = (got_rows.astype(f32) * mold_rows.astype(f32) * gap).astype(bf16)
    projected = jnp.dot(flux, wj, preferred_element_type=f32)
    lane = lax.broadcasted_iota(jnp.int32, (slots, row_width), 1)
    answers = jnp.where(lane < node_count, projected, gap).astype(bf16)
    gained = projected[:, node_count:].astype(bf16)

    returned = lax.all_to_all(
        answers.reshape(devices, capacity, row_width), axes, 0, 0, tiled=True
    ).reshape(slots, row_width)
    totals = lax.dot_general(selector, gained, contract0, preferred_element_type=f32)
    quarter = face_rows // vol_count
    face_totals = totals.astype(bf16).reshape(vol_count, quarter * node_count // row_width, row_width)
    face_totals, returned = lax.optimization_barrier((face_totals, returned))
    casting_out = jnp.take(returned, slot_index, axis=0, mode="clip")

    relaid = lax.all_to_all(
        face_totals,
        "vol",
        split_axis=0,
        concat_axis=0,
        tiled=True,
    )
    heat = jnp.dot(volume, conduct, preferred_element_type=f32)
    settled = volume.astype(f32) - relax * heat
    settled, relaid = lax.optimization_barrier((settled, relaid))
    placed = relaid.reshape(face_rows, node_count).astype(f32)
    inject = jnp.concatenate([placed, jnp.zeros((face_rows, node_count), f32)], axis=1)
    mold_out = (settled + relax * inject).astype(bf16)
    return (casting_out, mold_out)


def solution(mesh):
    return jax.shard_map(
        local,
        mesh=mesh,
        in_specs=(
            P(("surf", "vol"), None),
            P(("surf", "vol"), None),
            P(("surf", "vol")),
            P(("surf", "vol"), None),
            P(),
            P(),
            P(),
            P(("surf", "vol"), None),
        ),
        out_specs=(P(("surf", "vol"), None), P(("surf", "vol"), None)),
        check_vma=False,
    )
```

```python
import jax
import jax.numpy as jnp
from jax import lax
from jax.sharding import PartitionSpec as P

relax = 0.5


def contact(rows, mold_rows, stacked, joined, node_count):
    pair_rows = jnp.concatenate([rows[:, :node_count], mold_rows[:, :node_count]], axis=1)
    gap_jump = jnp.dot(pair_rows, stacked, preferred_element_type=jnp.float32)
    heat_flux = (
        rows[:, node_count:].astype(jnp.float32)
        * mold_rows[:, node_count:].astype(jnp.float32)
        * gap_jump
    ).astype(jnp.bfloat16)
    projected = jnp.dot(heat_flux, joined, preferred_element_type=jnp.float32)
    answer = jnp.concatenate([projected[:, :node_count], gap_jump], axis=1).astype(jnp.bfloat16)
    gained = projected[:, node_count:].astype(jnp.bfloat16)
    return (answer, gained)


def local(casting, owner, face_id, mold_faces, mortar_d, mortar_m, conduct, volume):
    seg_rows, row_width = casting.shape
    node_count = mortar_d.shape[0]
    face_rows = mold_faces.shape[0]
    surf_count = lax.axis_size("surf")
    vol_count = lax.axis_size("vol")
    devices = surf_count * vol_count
    capacity = 4 * seg_rows // devices
    slots = devices * capacity
    axes = ("surf", "vol")
    f32, bf16 = jnp.float32, jnp.bfloat16
    contract0 = (((0,), (0,)), ((), ()))

    target = owner[:, 0]
    hits = (target[:, None] == jnp.arange(devices, dtype=jnp.int32)[None, :]).astype(bf16)
    row_i = lax.broadcasted_iota(jnp.int32, (seg_rows, seg_rows), 0)
    row_j = lax.broadcasted_iota(jnp.int32, (seg_rows, seg_rows), 1)
    earlier = (row_j < row_i).astype(bf16)
    before = jnp.dot(earlier, hits, preferred_element_type=f32)
    position = jnp.sum(before * hits.astype(f32), axis=1).astype(jnp.int32)
    slot_index = target * capacity + position

    code = face_id + 1
    pos_hot = (position[:, None] == jnp.arange(capacity, dtype=jnp.int32)[None, :]).astype(bf16)
    hi = (code // 64).astype(bf16)[:, None]
    lo = (code % 64).astype(bf16)[:, None]
    id_count = 2 * capacity
    id_height = -(-id_count // row_width)
    codes = jnp.concatenate([pos_hot * hi, pos_hot * lo], axis=1)
    id_flat = lax.dot_general(hits, codes, contract0, preferred_element_type=f32)
    id_flat = jnp.pad(id_flat, ((0, 0), (0, id_height * row_width - id_count)))
    id_rows = id_flat.reshape(devices, id_height, row_width)

    send_rows = jnp.zeros((slots, row_width), bf16).at[slot_index].set(casting)
    send = jnp.concatenate(
        [send_rows.reshape(devices, capacity, row_width), id_rows.astype(bf16)], axis=1
    )
    got = lax.all_to_all(send, axes, 0, 0, tiled=True)
    got_rows = got[:, :capacity, :].reshape(slots, row_width)
    got_code = got[:, capacity:, :].astype(f32).reshape(devices, id_height * row_width)
    got_code = got_code[:, :id_count].reshape(devices, 2, capacity)
    got_ids = (got_code[:, 0, :] * 64.0 + got_code[:, 1, :]).astype(jnp.int32).reshape(slots) - 1

    face_range = jnp.arange(face_rows, dtype=jnp.int32)
    selector_t = (face_range[:, None] == got_ids[None, :]).astype(bf16)
    mold_rows = lax.dot_general(
        selector_t, mold_faces, contract0, preferred_element_type=f32
    ).astype(bf16)

    zero = jnp.zeros((node_count, node_count), bf16)
    wc = jnp.block([[zero, mortar_d.T], [zero, zero]])
    wm = jnp.block([[zero, -mortar_m.T], [zero, zero]])
    wj = jnp.block([[zero, zero], [mortar_d, mortar_m]])
    gap = jnp.dot(got_rows, wc, preferred_element_type=f32) + jnp.dot(
        mold_rows, wm, preferred_element_type=f32
    )
    flux = (got_rows.astype(f32) * mold_rows.astype(f32) * gap).astype(bf16)
    projected = jnp.dot(flux, wj, preferred_element_type=f32)
    lane = lax.broadcasted_iota(jnp.int32, (slots, row_width), 1)
    answers = jnp.where(lane < node_count, projected, gap).astype(bf16)
    gained = projected[:, node_count:].astype(bf16)

    returned = lax.all_to_all(
        answers.reshape(devices, capacity, row_width), axes, 0, 0, tiled=True
    ).reshape(slots, row_width)
    totals = jnp.dot(selector_t, gained, preferred_element_type=f32)
    quarter = face_rows // vol_count
    face_totals = totals.astype(bf16).reshape(vol_count, quarter * node_count // row_width, row_width)
    face_totals, returned = lax.optimization_barrier((face_totals, returned))
    casting_out = jnp.take(returned, slot_index, axis=0, mode="clip")

    relaid = lax.all_to_all(
        face_totals,
        "vol",
        split_axis=0,
        concat_axis=0,
        tiled=True,
    )
    heat = jnp.dot(volume, conduct, preferred_element_type=f32)
    settled = volume.astype(f32) - relax * heat
    settled, relaid = lax.optimization_barrier((settled, relaid))
    placed = relaid.reshape(face_rows, node_count).astype(f32)
    inject = jnp.concatenate([placed, jnp.zeros((face_rows, node_count), f32)], axis=1)
    mold_out = (settled + relax * inject).astype(bf16)
    return (casting_out, mold_out)


def solution(mesh):
    return jax.shard_map(
        local,
        mesh=mesh,
        in_specs=(
            P(("surf", "vol"), None),
            P(("surf", "vol"), None),
            P(("surf", "vol")),
            P(("surf", "vol"), None),
            P(),
            P(),
            P(),
            P(("surf", "vol"), None),
        ),
        out_specs=(P(("surf", "vol"), None), P(("surf", "vol"), None)),
        check_vma=False,
    )
```

```python
import jax
import jax.numpy as jnp
from jax import lax
from jax.sharding import PartitionSpec as P

relax = 0.5


def contact(rows, mold_rows, stacked, joined, node_count):
    pair_rows = jnp.concatenate([rows[:, :node_count], mold_rows[:, :node_count]], axis=1)
    gap_jump = jnp.dot(pair_rows, stacked, preferred_element_type=jnp.float32)
    heat_flux = (
        rows[:, node_count:].astype(jnp.float32)
        * mold_rows[:, node_count:].astype(jnp.float32)
        * gap_jump
    ).astype(jnp.bfloat16)
    projected = jnp.dot(heat_flux, joined, preferred_element_type=jnp.float32)
    answer = jnp.concatenate([projected[:, :node_count], gap_jump], axis=1).astype(jnp.bfloat16)
    gained = projected[:, node_count:].astype(jnp.bfloat16)
    return (answer, gained)


def local(casting, owner, face_id, mold_faces, mortar_d, mortar_m, conduct, volume):
    seg_rows, row_width = casting.shape
    node_count = mortar_d.shape[0]
    face_rows = mold_faces.shape[0]
    surf_count = lax.axis_size("surf")
    vol_count = lax.axis_size("vol")
    devices = surf_count * vol_count
    capacity = 4 * seg_rows // devices
    slots = devices * capacity
    axes = ("surf", "vol")
    f32, bf16 = jnp.float32, jnp.bfloat16
    contract0 = (((0,), (0,)), ((), ()))

    target = owner[:, 0]
    hits = (target[:, None] == jnp.arange(devices, dtype=jnp.int32)[None, :]).astype(bf16)
    row_i = lax.broadcasted_iota(jnp.int32, (seg_rows, seg_rows), 0)
    row_j = lax.broadcasted_iota(jnp.int32, (seg_rows, seg_rows), 1)
    earlier = (row_j < row_i).astype(bf16)
    before = jnp.dot(earlier, hits, preferred_element_type=f32)
    position = jnp.sum(before * hits.astype(f32), axis=1).astype(jnp.int32)
    slot_index = target * capacity + position

    code = face_id + 1
    pos_hot = (position[:, None] == jnp.arange(capacity, dtype=jnp.int32)[None, :]).astype(bf16)
    hi = (code // 64).astype(bf16)[:, None]
    lo = (code % 64).astype(bf16)[:, None]
    id_count = 2 * capacity
    id_height = -(-id_count // row_width)
    codes = jnp.concatenate([pos_hot * hi, pos_hot * lo], axis=1)
    id_flat = lax.dot_general(hits, codes, contract0, preferred_element_type=f32)
    id_flat = jnp.pad(id_flat, ((0, 0), (0, id_height * row_width - id_count)))
    id_rows = id_flat.reshape(devices, id_height, row_width)

    send_rows = jnp.zeros((slots, row_width), bf16).at[slot_index].set(casting)
    send = jnp.concatenate(
        [send_rows.reshape(devices, capacity, row_width), id_rows.astype(bf16)], axis=1
    )
    got = lax.all_to_all(send, axes, 0, 0, tiled=True)
    got_rows = got[:, :capacity, :].reshape(slots, row_width)
    got_code = got[:, capacity:, :].astype(f32).reshape(devices, id_height * row_width)
    got_code = got_code[:, :id_count].reshape(devices, 2, capacity)
    got_ids = (got_code[:, 0, :] * 64.0 + got_code[:, 1, :]).astype(jnp.int32).reshape(slots) - 1

    face_range = jnp.arange(face_rows, dtype=jnp.int32)
    selector = (got_ids[:, None] == face_range[None, :]).astype(bf16)
    mold_rows = jnp.dot(selector, mold_faces, preferred_element_type=f32).astype(bf16)

    zero = jnp.zeros((node_count, node_count), bf16)
    wc = jnp.block([[zero, mortar_d.T], [zero, zero]])
    wm = jnp.block([[zero, -mortar_m.T], [zero, zero]])
    wj = jnp.block([[zero, zero], [mortar_d, mortar_m]])
    gap = jnp.dot(got_rows, wc, preferred_element_type=f32) + jnp.dot(
        mold_rows, wm, preferred_element_type=f32
    )
    flux = (got_rows.astype(f32) * mold_rows.astype(f32) * gap).astype(bf16)
    projected = jnp.dot(flux, wj, preferred_element_type=f32)
    lane = lax.broadcasted_iota(jnp.int32, (slots, row_width), 1)
    answers = jnp.where(lane < node_count, projected, gap).astype(bf16)
    gained = projected[:, node_count:].astype(bf16)

    returned = lax.all_to_all(
        answers.reshape(devices, capacity, row_width), axes, 0, 0, tiled=True
    ).reshape(slots, row_width)
    totals = lax.dot_general(selector, gained, contract0, preferred_element_type=f32)
    quarter = face_rows // vol_count
    face_totals = totals.astype(bf16).reshape(vol_count, quarter * node_count // row_width, row_width)
    face_totals, returned = lax.optimization_barrier((face_totals, returned))
    casting_out = returned.at[slot_index].get(mode="promise_in_bounds")

    relaid = lax.all_to_all(
        face_totals,
        "vol",
        split_axis=0,
        concat_axis=0,
        tiled=True,
    )
    heat = jnp.dot(volume, conduct, preferred_element_type=f32)
    settled = volume.astype(f32) - relax * heat
    settled, relaid = lax.optimization_barrier((settled, relaid))
    placed = relaid.reshape(face_rows, node_count).astype(f32)
    inject = jnp.concatenate([placed, jnp.zeros((face_rows, node_count), f32)], axis=1)
    mold_out = (settled + relax * inject).astype(bf16)
    return (casting_out, mold_out)


def solution(mesh):
    return jax.shard_map(
        local,
        mesh=mesh,
        in_specs=(
            P(("surf", "vol"), None),
            P(("surf", "vol"), None),
            P(("surf", "vol")),
            P(("surf", "vol"), None),
            P(),
            P(),
            P(),
            P(("surf", "vol"), None),
        ),
        out_specs=(P(("surf", "vol"), None), P(("surf", "vol"), None)),
        check_vma=False,
    )
```

```python
import jax
import jax.numpy as jnp
from jax import lax
from jax.sharding import PartitionSpec as P

relax = 0.5


def contact(rows, mold_rows, stacked, joined, node_count):
    pair_rows = jnp.concatenate([rows[:, :node_count], mold_rows[:, :node_count]], axis=1)
    gap_jump = jnp.dot(pair_rows, stacked, preferred_element_type=jnp.float32)
    heat_flux = (
        rows[:, node_count:].astype(jnp.float32)
        * mold_rows[:, node_count:].astype(jnp.float32)
        * gap_jump
    ).astype(jnp.bfloat16)
    projected = jnp.dot(heat_flux, joined, preferred_element_type=jnp.float32)
    answer = jnp.concatenate([projected[:, :node_count], gap_jump], axis=1).astype(jnp.bfloat16)
    gained = projected[:, node_count:].astype(jnp.bfloat16)
    return (answer, gained)


def local(casting, owner, face_id, mold_faces, mortar_d, mortar_m, conduct, volume):
    seg_rows, row_width = casting.shape
    node_count = mortar_d.shape[0]
    face_rows = mold_faces.shape[0]
    surf_count = lax.axis_size("surf")
    vol_count = lax.axis_size("vol")
    devices = surf_count * vol_count
    capacity = 4 * seg_rows // devices
    slots = devices * capacity
    axes = ("surf", "vol")
    f32, bf16 = jnp.float32, jnp.bfloat16
    contract0 = (((0,), (0,)), ((), ()))

    target = owner[:, 0]
    hits = (target[:, None] == jnp.arange(devices, dtype=jnp.int32)[None, :]).astype(bf16)
    row_i = lax.broadcasted_iota(jnp.int32, (seg_rows, seg_rows), 0)
    row_j = lax.broadcasted_iota(jnp.int32, (seg_rows, seg_rows), 1)
    same = (row_j < row_i) & (target[None, :] == target[:, None])
    position = jnp.sum(same.astype(jnp.int32), axis=1)
    slot_index = target * capacity + position

    code = face_id + 1
    pos_hot = (position[:, None] == jnp.arange(capacity, dtype=jnp.int32)[None, :]).astype(bf16)
    hi = (code // 64).astype(bf16)[:, None]
    lo = (code % 64).astype(bf16)[:, None]
    id_count = 2 * capacity
    id_height = -(-id_count // row_width)
    codes = jnp.concatenate([pos_hot * hi, pos_hot * lo], axis=1)
    id_flat = lax.dot_general(hits, codes, contract0, preferred_element_type=f32)
    id_flat = jnp.pad(id_flat, ((0, 0), (0, id_height * row_width - id_count)))
    id_rows = id_flat.reshape(devices, id_height, row_width)

    send_rows = jnp.zeros((slots, row_width), bf16).at[slot_index].set(casting)
    send = jnp.concatenate(
        [send_rows.reshape(devices, capacity, row_width), id_rows.astype(bf16)], axis=1
    )
    got = lax.all_to_all(send, axes, 0, 0, tiled=True)
    got_rows = got[:, :capacity, :].reshape(slots, row_width)
    got_code = got[:, capacity:, :].astype(f32).reshape(devices, id_height * row_width)
    got_code = got_code[:, :id_count].reshape(devices, 2, capacity)
    got_ids = (got_code[:, 0, :] * 64.0 + got_code[:, 1, :]).astype(jnp.int32).reshape(slots) - 1

    face_range = jnp.arange(face_rows, dtype=jnp.int32)
    selector = (got_ids[:, None] == face_range[None, :]).astype(bf16)
    mold_rows = jnp.dot(selector, mold_faces, preferred_element_type=f32).astype(bf16)

    zero = jnp.zeros((node_count, node_count), bf16)
    wc = jnp.block([[zero, mortar_d.T], [zero, zero]])
    wm = jnp.block([[zero, -mortar_m.T], [zero, zero]])
    wj = jnp.block([[zero, zero], [mortar_d, mortar_m]])
    gap = jnp.dot(got_rows, wc, preferred_element_type=f32) + jnp.dot(
        mold_rows, wm, preferred_element_type=f32
    )
    flux = (got_rows.astype(f32) * mold_rows.astype(f32) * gap).astype(bf16)
    projected = jnp.dot(flux, wj, preferred_element_type=f32)
    lane = lax.broadcasted_iota(jnp.int32, (slots, row_width), 1)
    answers = jnp.where(lane < node_count, projected, gap).astype(bf16)
    gained = projected[:, node_count:].astype(bf16)

    returned = lax.all_to_all(
        answers.reshape(devices, capacity, row_width), axes, 0, 0, tiled=True
    ).reshape(slots, row_width)
    totals = lax.dot_general(selector, gained, contract0, preferred_element_type=f32)
    quarter = face_rows // vol_count
    face_totals = totals.astype(bf16).reshape(vol_count, quarter * node_count // row_width, row_width)
    face_totals, returned = lax.optimization_barrier((face_totals, returned))
    casting_out = jnp.take(returned, slot_index, axis=0, mode="clip")

    relaid = lax.all_to_all(
        face_totals,
        "vol",
        split_axis=0,
        concat_axis=0,
        tiled=True,
    )
    heat = jnp.dot(volume, conduct, preferred_element_type=f32)
    settled = volume.astype(f32) - relax * heat
    settled, relaid = lax.optimization_barrier((settled, relaid))
    placed = relaid.reshape(face_rows, node_count).astype(f32)
    inject = jnp.concatenate([placed, jnp.zeros((face_rows, node_count), f32)], axis=1)
    mold_out = (settled + relax * inject).astype(bf16)
    return (casting_out, mold_out)


def solution(mesh):
    return jax.shard_map(
        local,
        mesh=mesh,
        in_specs=(
            P(("surf", "vol"), None),
            P(("surf", "vol"), None),
            P(("surf", "vol")),
            P(("surf", "vol"), None),
            P(),
            P(),
            P(),
            P(("surf", "vol"), None),
        ),
        out_specs=(P(("surf", "vol"), None), P(("surf", "vol"), None)),
        check_vma=False,
    )
```
